32 devices in a mesh: gx: 8 (over z, core), gy: 4 (over y, x).
Axes of the slice: x: 2, y: 2, z: 4, core: 2. Of those that a mesh axis runs over, the one named last changes fastest.
Arguments:
- gap: float32 [8, 4, 896, 128], P('gx', 'gy'), may hold values from -6 to 6
- own_rows: float32 [8, 4, 640, 896], P('gx', 'gy')
- spill_rows: float32 [8, 4, 2, 128, 896], P('gx', 'gy')
- tile_plan: int32 [8, 4, 2], P('gx', 'gy'), may hold values from -1 to 6, as said below
- orders: int32 [8, 4], P('gx', 'gy'), may hold values from 384 to 896, as said below
- slot_rows: int32 [8, 4, 896], P('gx', 'gy'), may hold values from 0 to 895, each once within a row
Outputs:
- solution: float32 [8, 4, 896, 128], P('gx', 'gy')
- residual: float32 [8, 4, 896, 128], P('gx', 'gy')
The draws below stay inside these ranges and needn't reach their ends.
Inputs may be any that keep to these rules, and one draw needn't show every extreme that they name: `orders`: the largest order, 896, is taken by some subdomain in every draw. `tile_plan`: for subdomain (i, j) and slot s, the index of the row tile of its operator stored in slot s of spill_rows on subdomain ((i + (s + 1) * 2) mod 8, j), or -1. Every tile from 5 on that holds rows under the subdomain's order sits in exactly one slot, and no other tile does. `slot_rows`: for each subdomain a permutation of its operator rows over its slots.
All inputs are finite; a program needn't handle non-finite values.
Results may differ from the reference program's by a relative error of at most 0.0003.
Values sent between devices are 32-bit elements; how exact they have to be, the bound alone decides.
No kernel may reach another device: no remote copies, remote signals or barrier semaphores. Data moves between devices by JAX's collectives and lax.ppermute only.
A program may use at most 64 MiB of HBM per device.

```python
import math
import jax
import jax.numpy as jnp
from jax import lax

M = 896
TILE = 128
K = 128
ITERS = 4
OWN_T = 5
ORD_LO = 384
HOP = 2
SUBX = 8
SUBY = 4


def plan_orders(key):
    base = jax.random.fold_in(key, 101)
    first_key, second_key = jax.random.split(base)
    values = jax.random.randint(first_key, (SUBX * SUBY,), ORD_LO, M + 1)
    spot = jax.random.randint(second_key, (), 0, SUBX * SUBY)
    values = jnp.where(jnp.arange(SUBX * SUBY) == spot, M, values)
    return values.reshape(SUBX, SUBY).astype(jnp.int32)


def plan_tiles(key):
    order_vals = plan_orders(key)
    own_tiles = M // TILE - 2
    extra = (order_vals + TILE - 1) // TILE - own_tiles
    flip = jax.random.randint(jax.random.fold_in(key, 202), (SUBX, SUBY), 0, 2)
    first_slot = jnp.where(extra >= 2, jnp.where(flip == 0, own_tiles, own_tiles + 1), jnp.where((extra == 1) & (flip == 0), own_tiles, -1))
    second_slot = jnp.where(extra >= 2, jnp.where(flip == 0, own_tiles + 1, own_tiles), jnp.where((extra == 1) & (flip == 1), own_tiles, -1))
    return jnp.stack([first_slot, second_slot], axis=-1).astype(jnp.int32)


def operator_noise(key, shape):
    noise_key, diag_key = jax.random.split(key)
    off_part = jax.random.normal(noise_key, shape, jnp.float32) * (0.5 / math.sqrt(M))
    diag_part = jax.random.uniform(diag_key, shape[:-1], jnp.float32, 1.0, 2.5)
    return (off_part, diag_part)


def draw_orders(key, part):
    return plan_orders(key)


def draw_tile_plan(key, part):
    return plan_tiles(key)


def draw_own_rows(key, part):
    own_count = M - 2 * TILE
    off_part, diag_part = operator_noise(jax.random.fold_in(key, 303), (SUBX, SUBY, own_count, M))
    row_ids = jnp.arange(own_count)[:, None]
    col_ids = jnp.arange(M)[None, :]
    return (off_part + jnp.where(row_ids == col_ids, diag_part[..., None], 0.0)).astype(jnp.float32)


def draw_spill_rows(key, part):
    plan_vals = plan_tiles(key)
    owner_tile = jnp.stack([jnp.roll(plan_vals[:, :, slot_id], (slot_id + 1) * HOP, axis=0) for slot_id in range(2)], axis=2)
    off_part, diag_part = operator_noise(jax.random.fold_in(key, 404), (SUBX, SUBY, 2, TILE, M))
    target = owner_tile[:, :, :, None, None] * TILE + jnp.arange(TILE)[:, None]
    col_ids = jnp.arange(M)[None, :]
    return (off_part + jnp.where(col_ids == target, diag_part[..., None], 0.0)).astype(jnp.float32)


def level_of(rng, extent, pieces, low, top_value):
    factor_of, own = 1.0, jax.random.fold_in(rng, 6)
    for dim, shards_of in pieces:
        heights = jnp.exp(jax.random.uniform(jax.random.fold_in(own, dim), (shards_of,), jnp.float32, low / len(pieces), top_value / len(pieces)))
        factor_of = factor_of * jnp.repeat(heights, extent[dim] // shards_of).reshape([-1 if axis == dim else 1 for axis in range(len(extent))])
    return factor_of


def bell_draw(stream_key, extent, scale, reach, pieces=(), dtype=jnp.bfloat16):
    drawn = jax.random.normal(stream_key, extent, jnp.float32) * scale
    if len(pieces) > 0:
        drawn = level_of(stream_key, extent, pieces, -0.22, 0.18) * drawn
    return jnp.clip(drawn, min=-reach, max=reach).astype(dtype)


def setup_inputs(seed: int = 0) -> dict:
    keys = jax.random.split(jax.random.key(seed), 7)
    return {
        "gap": bell_draw(keys[0], (SUBX, SUBY, M, K), 1.0, 6.0, ((0, 8), (1, 4)), jnp.float32),
        "own_rows": draw_own_rows(jax.random.fold_in(keys[6], 71), 0),
        "spill_rows": draw_spill_rows(jax.random.fold_in(keys[6], 71), 0),
        "tile_plan": draw_tile_plan(jax.random.fold_in(keys[6], 71), 0),
        "orders": draw_orders(jax.random.fold_in(keys[6], 71), 0),
        "slot_rows": jax.vmap(lambda own: jax.random.permutation(own, M))(jax.random.split(keys[5], SUBX * SUBY)).reshape((SUBX, SUBY, M)).astype(jnp.int32),
    }


low_bound = 0.5
high_bound = 7.0


def face_signs(order_max):
    slot_ids = jnp.arange(order_max).astype(jnp.int32)
    return jnp.where((slot_ids // (order_max // 4)) % 2 == 0, -1.0, 1.0).astype(jnp.float32)


def assemble(local):
    width = local.shape[2] // 4
    low_x = local[:, :, 0:width]
    high_x = local[:, :, width:2 * width]
    low_y = local[:, :, 2 * width:3 * width]
    high_y = local[:, :, 3 * width:4 * width]
    zero_x = jnp.zeros_like(low_x[:1])
    zero_y = jnp.zeros_like(low_y[:, :1])
    new_low_x = low_x + jnp.concatenate([zero_x, high_x[:-1]], axis=0)
    new_high_x = high_x + jnp.concatenate([low_x[1:], zero_x], axis=0)
    new_low_y = low_y + jnp.concatenate([zero_y, high_y[:, :-1]], axis=1)
    new_high_y = high_y + jnp.concatenate([low_y[:, 1:], zero_y], axis=1)
    return jnp.concatenate([new_low_x, new_high_x, new_low_y, new_high_y], axis=2)


def extra_tiles(spill_rows, tile_plan):
    rolled = [jnp.roll(spill_rows[:, :, slot_id], -(slot_id + 1) * HOP, axis=0) for slot_id in range(2)]
    tiles = []
    for extra_id in range(2):
        gathered = jnp.zeros_like(rolled[0])
        for slot_id in range(2):
            match = (tile_plan[:, :, slot_id] == OWN_T + extra_id)[:, :, None, None]
            gathered = gathered + jnp.where(match, rolled[slot_id], 0.0)
        tiles.append(gathered)
    return jnp.concatenate(tiles, axis=2)


def apply_operator(field, own_rows, extra_rows, orders, slot_rows):
    face_sign = face_signs(M)
    count = SUBX * SUBY

    def per_subdomain(operands):
        values, own_block, extra_block, order_now, slot_map = operands
        operator = jnp.concatenate([own_block, extra_block], axis=0)
        row_ids = jnp.arange(M).astype(jnp.int32)
        slot_of_row = jnp.zeros((M,), jnp.int32).at[slot_map].set(row_ids)
        live_rows = (row_ids < order_now).astype(jnp.float32)[:, None]
        multipliers = values[slot_of_row] * (face_sign[slot_of_row][:, None] * live_rows)
        result = jnp.dot(operator, multipliers, precision=lax.Precision.HIGHEST, preferred_element_type=jnp.float32) * live_rows
        return result[slot_map] * face_sign[:, None]

    local = lax.map(per_subdomain, (field.reshape(count, M, K), own_rows.reshape(count, OWN_T * TILE, M), extra_rows.reshape(count, 2 * TILE, M), orders.reshape(count), slot_rows.reshape(count, M)))
    return assemble(local.reshape(SUBX, SUBY, M, K))


def reference(gap, own_rows, spill_rows, tile_plan, orders, slot_rows):
    extra_rows = extra_tiles(spill_rows, tile_plan)
    load = assemble(gap)
    centre = (high_bound + low_bound) / 2.0
    half_width = (high_bound - low_bound) / 2.0
    sigma_value = centre / half_width
    rho_value = 1.0 / sigma_value
    solution = jnp.zeros_like(load)
    residual = load
    direction = residual / centre
    for step_id in range(ITERS):
        solution = solution + direction
        residual = residual - apply_operator(direction, own_rows, extra_rows, orders, slot_rows)
        if step_id + 1 < ITERS:
            rho_next = 1.0 / (2.0 * sigma_value - rho_value)
            direction = (rho_next * rho_value) * direction + (2.0 * rho_next / half_width) * residual
            rho_value = rho_next
    return solution, residual
```

```python
import jax
import jax.numpy as jnp
from jax import lax
from jax.sharding import PartitionSpec as P

ITERS = 4


low_bound = 0.5
high_bound = 7.0


def shifted(block, axis, distance):
    devices = range(lax.axis_size(axis))
    route = [(i - distance, i) for i in devices if i - distance in devices]
    return lax.ppermute(block, axis, route)


def from_behind(value, axis, steps):
    count = lax.axis_size(axis)
    pairs = [(source, (source + steps) % count) for source in range(count)]
    return lax.ppermute(value, axis, pairs)


def along_x(part, offset):
    return shifted(part, "gx", offset)


def along_y(part, offset):
    return shifted(part, "gy", offset)


def face_sum(local):
    width = local.shape[0] // 4
    low_x = local[0:width]
    high_x = local[width : 2 * width]
    low_y = local[2 * width : 3 * width]
    high_y = local[3 * width : 4 * width]
    return jnp.concatenate(
        [
            low_x + along_x(high_x, 1),
            high_x + along_x(low_x, -1),
            low_y + along_y(high_y, 1),
            high_y + along_y(low_y, -1),
        ],
        axis=0,
    )


def body(gap, own_rows, spill_rows, tile_plan, orders, slot_rows):
    order_max = gap.shape[2]
    tile_rows = spill_rows.shape[3]
    own_tiles = own_rows.shape[2] // tile_rows
    hop_span = lax.axis_size("gx") // 4
    own_block = own_rows[0, 0]
    spill_block = spill_rows[0, 0]
    plan_row = tile_plan[0, 0]
    order_now = orders[0, 0]
    slot_map = slot_rows[0, 0]
    row_ids = jnp.arange(order_max, dtype=jnp.int32)
    face_sign = jnp.where(row_ids // (order_max // 4) % 2 == 0, -1.0, 1.0).astype(jnp.float32)
    slot_scale = face_sign * (slot_map < order_now).astype(jnp.float32)
    homed = [
        from_behind(spill_block[slot_id], "gx", -(slot_id + 1) * hop_span) for slot_id in range(2)
    ]
    extra_rows = []
    for extra_id in range(2):
        gathered = jnp.zeros_like(homed[0])
        for slot_id in range(2):
            gathered = gathered + jnp.where(
                plan_row[slot_id] == own_tiles + extra_id, homed[slot_id], 0.0
            )
        extra_rows.append(gathered)
    operator = jnp.concatenate([own_block] + extra_rows, axis=0)
    by_rows = jnp.take(operator, slot_map, axis=0)
    by_cols = jnp.take(by_rows.T, slot_map, axis=0)
    slot_op = (by_cols * slot_scale[:, None]).T * slot_scale[:, None]
    load = face_sum(gap[0, 0])
    centre = (high_bound + low_bound) / 2.0
    half_width = (high_bound - low_bound) / 2.0
    sigma_value = centre / half_width
    rho_value = 1.0 / sigma_value
    solution = jnp.zeros_like(load)
    residual = load
    direction = residual / centre
    for step_id in range(ITERS):
        solution = solution + direction
        local = jnp.dot(
            slot_op,
            direction,
            precision=lax.Precision.HIGHEST,
            preferred_element_type=jnp.float32,
        )
        residual = residual - face_sum(local)
        if step_id + 1 < ITERS:
            rho_next = 1.0 / (2.0 * sigma_value - rho_value)
            direction = rho_next * rho_value * direction + 2.0 * rho_next / half_width * residual
            rho_value = rho_next
    return (solution[None, None], residual[None, None])


def solution(mesh):
    in_specs = (
        P("gx", "gy", None, None),
        P("gx", "gy", None, None),
        P("gx", "gy", None, None, None),
        P("gx", "gy", None),
        P("gx", "gy"),
        P("gx", "gy", None),
    )
    out_specs = (P("gx", "gy", None, None), P("gx", "gy", None, None))
    return jax.shard_map(body, mesh=mesh, in_specs=in_specs, out_specs=out_specs, check_vma=False)
```

```python
import jax
import jax.numpy as jnp
from jax import lax
from jax.sharding import PartitionSpec as P

ITERS = 4


low_bound = 0.5
high_bound = 7.0


def shifted(block, axis, distance):
    devices = range(lax.axis_size(axis))
    route = [(i - distance, i) for i in devices if i - distance in devices]
    return lax.ppermute(block, axis, route)


def from_behind(value, axis, steps):
    count = lax.axis_size(axis)
    pairs = [(source, (source + steps) % count) for source in range(count)]
    return lax.ppermute(value, axis, pairs)


def along_x(part, offset):
    return shifted(part, "gx", offset)


def along_y(part, offset):
    return shifted(part, "gy", offset)


def face_sum(local):
    width = local.shape[0] // 4
    low_x = local[0:width]
    high_x = local[width : 2 * width]
    low_y = local[2 * width : 3 * width]
    high_y = local[3 * width : 4 * width]
    return jnp.concatenate(
        [
            low_x + along_x(high_x, 1),
            high_x + along_x(low_x, -1),
            low_y + along_y(high_y, 1),
            high_y + along_y(low_y, -1),
        ],
        axis=0,
    )


def face_sum_parts(faces):
    low_x, high_x, low_y, high_y = faces
    return jnp.concatenate(
        [
            low_x + along_x(high_x, 1),
            high_x + along_x(low_x, -1),
            low_y + along_y(high_y, 1),
            high_y + along_y(low_y, -1),
        ],
        axis=0,
    )


def body(gap, own_rows, spill_rows, tile_plan, orders, slot_rows):
    order_max = gap.shape[2]
    tile_rows = spill_rows.shape[3]
    own_tiles = own_rows.shape[2] // tile_rows
    hop_span = lax.axis_size("gx") // 4
    own_block = own_rows[0, 0]
    spill_block = spill_rows[0, 0]
    plan_row = tile_plan[0, 0]
    order_now = orders[0, 0]
    slot_map = slot_rows[0, 0]
    row_ids = jnp.arange(order_max, dtype=jnp.int32)
    face_sign = jnp.where(row_ids // (order_max // 4) % 2 == 0, -1.0, 1.0).astype(jnp.float32)
    slot_scale = face_sign * (slot_map < order_now).astype(jnp.float32)
    homed = [
        from_behind(spill_block[slot_id], "gx", -(slot_id + 1) * hop_span) for slot_id in range(2)
    ]
    extra_rows = []
    for extra_id in range(2):
        gathered = jnp.zeros_like(homed[0])
        for slot_id in range(2):
            gathered = gathered + jnp.where(
                plan_row[slot_id] == own_tiles + extra_id, homed[slot_id], 0.0
            )
        extra_rows.append(gathered)
    operator = jnp.concatenate([own_block] + extra_rows, axis=0)
    by_rows = jnp.take(operator, slot_map, axis=0)
    by_cols = jnp.take(by_rows.T, slot_map, axis=0)
    slot_op = (by_cols * slot_scale[:, None]).T * slot_scale[:, None]
    load = face_sum(gap[0, 0])
    centre = (high_bound + low_bound) / 2.0
    half_width = (high_bound - low_bound) / 2.0
    sigma_value = centre / half_width
    rho_value = 1.0 / sigma_value
    solution = jnp.zeros_like(load)
    residual = load
    direction = residual / centre
    for step_id in range(ITERS):
        solution = solution + direction
        width = order_max // 4
        faces = [
            jnp.dot(
                slot_op[face_id * width : (face_id + 1) * width],
                direction,
                precision=lax.Precision.HIGH,
                preferred_element_type=jnp.float32,
            )
            for face_id in range(4)
        ]
        residual = residual - face_sum_parts(faces)
        if step_id + 1 < ITERS:
            rho_next = 1.0 / (2.0 * sigma_value - rho_value)
            direction = rho_next * rho_value * direction + 2.0 * rho_next / half_width * residual
            rho_value = rho_next
    return (solution[None, None], residual[None, None])


def solution(mesh):
    in_specs = (
        P("gx", "gy", None, None),
        P("gx", "gy", None, None),
        P("gx", "gy", None, None, None),
        P("gx", "gy", None),
        P("gx", "gy"),
        P("gx", "gy", None),
    )
    out_specs = (P("gx", "gy", None, None), P("gx", "gy", None, None))
    return jax.shard_map(body, mesh=mesh, in_specs=in_specs, out_specs=out_specs, check_vma=False)
```

```python
import jax
import jax.numpy as jnp
from jax import lax
from jax.sharding import PartitionSpec as P

ITERS = 4


low_bound = 0.5
high_bound = 7.0


def shifted(block, axis, distance):
    devices = range(lax.axis_size(axis))
    route = [(i - distance, i) for i in devices if i - distance in devices]
    return lax.ppermute(block, axis, route)


def from_behind(value, axis, steps):
    count = lax.axis_size(axis)
    pairs = [(source, (source + steps) % count) for source in range(count)]
    return lax.ppermute(value, axis, pairs)


def along_x(part, offset):
    return shifted(part, "gx", offset)


def along_y(part, offset):
    return shifted(part, "gy", offset)


def face_sum(local):
    width = local.shape[0] // 4
    low_x = local[0:width]
    high_x = local[width : 2 * width]
    low_y = local[2 * width : 3 * width]
    high_y = local[3 * width : 4 * width]
    return jnp.concatenate(
        [
            low_x + along_x(high_x, 1),
            high_x + along_x(low_x, -1),
            low_y + along_y(high_y, 1),
            high_y + along_y(low_y, -1),
        ],
        axis=0,
    )


def swap_pairs(count, first):
    pairs = []
    for low in range(first, count - 1, 2):
        pairs += [(low, low + 1), (low + 1, low)]
    return pairs


def axis_exchange(low, high, axis):
    count = lax.axis_size(axis)
    even = lax.axis_index(axis) % 2 == 0
    odd_recv = lax.ppermute(jnp.where(even, low, high), axis, swap_pairs(count, 1))
    even_recv = lax.ppermute(jnp.where(even, high, low), axis, swap_pairs(count, 0))
    new_low = low + jnp.where(even, odd_recv, even_recv)
    new_high = high + jnp.where(even, even_recv, odd_recv)
    return new_low, new_high


def face_sum_parts(faces):
    low_x, high_x, low_y, high_y = faces
    new_low_y, new_high_y = axis_exchange(low_y, high_y, "gy")
    new_low_x, new_high_x = axis_exchange(low_x, high_x, "gx")
    return jnp.concatenate([new_low_x, new_high_x, new_low_y, new_high_y], axis=0)


def body(gap, own_rows, spill_rows, tile_plan, orders, slot_rows):
    order_max = gap.shape[2]
    tile_rows = spill_rows.shape[3]
    own_tiles = own_rows.shape[2] // tile_rows
    hop_span = lax.axis_size("gx") // 4
    own_block = own_rows[0, 0]
    spill_block = spill_rows[0, 0]
    plan_row = tile_plan[0, 0]
    order_now = orders[0, 0]
    slot_map = slot_rows[0, 0]
    row_ids = jnp.arange(order_max, dtype=jnp.int32)
    face_sign = jnp.where(row_ids // (order_max // 4) % 2 == 0, -1.0, 1.0).astype(jnp.float32)
    slot_scale = face_sign * (slot_map < order_now).astype(jnp.float32)
    homed = [
        from_behind(spill_block[slot_id], "gx", -(slot_id + 1) * hop_span) for slot_id in range(2)
    ]
    extra_rows = []
    for extra_id in range(2):
        gathered = jnp.zeros_like(homed[0])
        for slot_id in range(2):
            gathered = gathered + jnp.where(
                plan_row[slot_id] == own_tiles + extra_id, homed[slot_id], 0.0
            )
        extra_rows.append(gathered)
    operator = jnp.concatenate([own_block] + extra_rows, axis=0)
    by_rows = jnp.take(operator, slot_map, axis=0)
    by_cols = jnp.take(by_rows.T, slot_map, axis=0)
    slot_op = (by_cols * slot_scale[:, None]).T * slot_scale[:, None]
    width = order_max // 4
    load = face_sum_parts([gap[0, 0, face_id * width : (face_id + 1) * width] for face_id in range(4)])
    centre = (high_bound + low_bound) / 2.0
    half_width = (high_bound - low_bound) / 2.0
    sigma_value = centre / half_width
    rho_value = 1.0 / sigma_value
    solution = jnp.zeros_like(load)
    residual = load
    direction = residual / centre
    for step_id in range(ITERS):
        solution = solution + direction
        width = order_max // 4
        faces = [
            jnp.dot(
                slot_op[face_id * width : (face_id + 1) * width],
                direction,
                precision=lax.Precision.HIGH,
                preferred_element_type=jnp.float32,
            )
            for face_id in range(4)
        ]
        residual = residual - face_sum_parts(faces)
        if step_id + 1 < ITERS:
            rho_next = 1.0 / (2.0 * sigma_value - rho_value)
            direction = rho_next * rho_value * direction + 2.0 * rho_next / half_width * residual
            rho_value = rho_next
    return (solution[None, None], residual[None, None])


def solution(mesh):
    in_specs = (
        P("gx", "gy", None, None),
        P("gx", "gy", None, None),
        P("gx", "gy", None, None, None),
        P("gx", "gy", None),
        P("gx", "gy"),
        P("gx", "gy", None),
    )
    out_specs = (P("gx", "gy", None, None), P("gx", "gy", None, None))
    return jax.shard_map(body, mesh=mesh, in_specs=in_specs, out_specs=out_specs, check_vma=False)
```

```python
import jax
import jax.numpy as jnp
from jax import lax
from jax.sharding import PartitionSpec as P

ITERS = 4


low_bound = 0.5
high_bound = 7.0


def shifted(block, axis, distance):
    devices = range(lax.axis_size(axis))
    route = [(i - distance, i) for i in devices if i - distance in devices]
    return lax.ppermute(block, axis, route)


def from_behind(value, axis, steps):
    count = lax.axis_size(axis)
    pairs = [(source, (source + steps) % count) for source in range(count)]
    return lax.ppermute(value, axis, pairs)


def along_x(part, offset):
    return shifted(part, "gx", offset)


def along_y(part, offset):
    return shifted(part, "gy", offset)


def face_sum(local):
    width = local.shape[0] // 4
    low_x = local[0:width]
    high_x = local[width : 2 * width]
    low_y = local[2 * width : 3 * width]
    high_y = local[3 * width : 4 * width]
    return jnp.concatenate(
        [
            low_x + along_x(high_x, 1),
            high_x + along_x(low_x, -1),
            low_y + along_y(high_y, 1),
            high_y + along_y(low_y, -1),
        ],
        axis=0,
    )


def swap_pairs(count, first):
    pairs = []
    for low in range(first, count - 1, 2):
        pairs += [(low, low + 1), (low + 1, low)]
    return pairs


def axis_exchange(low, high, axis):
    count = lax.axis_size(axis)
    even = lax.axis_index(axis) % 2 == 0
    odd_recv = lax.ppermute(jnp.where(even, low, high), axis, swap_pairs(count, 1))
    even_recv = lax.ppermute(jnp.where(even, high, low), axis, swap_pairs(count, 0))
    new_low = low + jnp.where(even, odd_recv, even_recv)
    new_high = high + jnp.where(even, even_recv, odd_recv)
    return new_low, new_high


def face_sum_parts(faces):
    low_x, high_x, low_y, high_y = faces
    new_low_y, new_high_y = axis_exchange(low_y, high_y, "gy")
    new_low_x, new_high_x = axis_exchange(low_x, high_x, "gx")
    return jnp.concatenate([new_low_x, new_high_x, new_low_y, new_high_y], axis=0)


def body(gap, own_rows, spill_rows, tile_plan, orders, slot_rows):
    order_max = gap.shape[2]
    tile_rows = spill_rows.shape[3]
    own_tiles = own_rows.shape[2] // tile_rows
    hop_span = lax.axis_size("gx") // 4
    own_block = own_rows[0, 0]
    spill_block = spill_rows[0, 0]
    plan_row = tile_plan[0, 0]
    order_now = orders[0, 0]
    slot_map = slot_rows[0, 0]
    row_ids = jnp.arange(order_max, dtype=jnp.int32)
    face_sign = jnp.where(row_ids // (order_max // 4) % 2 == 0, -1.0, 1.0).astype(jnp.float32)
    slot_scale = face_sign * (slot_map < order_now).astype(jnp.float32)
    homed = [
        from_behind(spill_block[slot_id], "gx", -(slot_id + 1) * hop_span) for slot_id in range(2)
    ]
    own_count = own_block.shape[0]
    width = order_max // 4
    load = face_sum_parts([gap[0, 0, face_id * width : (face_id + 1) * width] for face_id in range(4)])
    own_cols = (jnp.take(own_block.T, slot_map, axis=0) * slot_scale[:, None]).T
    in_own = slot_map < own_count
    own_op = jnp.where(
        in_own[:, None], jnp.take(own_cols, jnp.minimum(slot_map, own_count - 1), axis=0), 0.0
    ) * slot_scale[:, None]
    extra_rows = []
    for extra_id in range(2):
        gathered = jnp.zeros_like(homed[0])
        for slot_id in range(2):
            gathered = gathered + jnp.where(
                plan_row[slot_id] == own_tiles + extra_id, homed[slot_id], 0.0
            )
        extra_rows.append(gathered)
    extra_block = jnp.concatenate(extra_rows, axis=0)
    extra_count = extra_block.shape[0]
    extra_cols = (jnp.take(extra_block.T, slot_map, axis=0) * slot_scale[:, None]).T
    extra_ids = jnp.arange(extra_count, dtype=jnp.int32)
    extra_place = jnp.where(
        (slot_map - own_count)[:, None] == extra_ids[None, :], slot_scale[:, None], 0.0
    )
    centre = (high_bound + low_bound) / 2.0
    half_width = (high_bound - low_bound) / 2.0
    sigma_value = centre / half_width
    rho_value = 1.0 / sigma_value
    solution = jnp.zeros_like(load)
    residual = load
    direction = residual / centre
    for step_id in range(ITERS):
        solution = solution + direction
        extra_out = jnp.dot(
            extra_cols, direction, precision=lax.Precision.HIGH, preferred_element_type=jnp.float32
        )
        faces = [
            jnp.dot(
                own_op[face_id * width : (face_id + 1) * width],
                direction,
                precision=lax.Precision.HIGH,
                preferred_element_type=jnp.float32,
            )
            + jnp.dot(
                extra_place[face_id * width : (face_id + 1) * width],
                extra_out,
                precision=lax.Precision.HIGHEST,
                preferred_element_type=jnp.float32,
            )
            for face_id in range(4)
        ]
        residual = residual - face_sum_parts(faces)
        if step_id + 1 < ITERS:
            rho_next = 1.0 / (2.0 * sigma_value - rho_value)
            direction = rho_next * rho_value * direction + 2.0 * rho_next / half_width * residual
            rho_value = rho_next
    return (solution[None, None], residual[None, None])


def solution(mesh):
    in_specs = (
        P("gx", "gy", None, None),
        P("gx", "gy", None, None),
        P("gx", "gy", None, None, None),
        P("gx", "gy", None),
        P("gx", "gy"),
        P("gx", "gy", None),
    )
    out_specs = (P("gx", "gy", None, None), P("gx", "gy", None, None))
    return jax.shard_map(body, mesh=mesh, in_specs=in_specs, out_specs=out_specs, check_vma=False)
```

```python
import jax
import jax.numpy as jnp
from jax import lax
from jax.sharding import PartitionSpec as P

ITERS = 4


low_bound = 0.5
high_bound = 7.0


def shifted(block, axis, distance):
    devices = range(lax.axis_size(axis))
    route = [(i - distance, i) for i in devices if i - distance in devices]
    return lax.ppermute(block, axis, route)


def from_behind(value, axis, steps):
    count = lax.axis_size(axis)
    pairs = [(source, (source + steps) % count) for source in range(count)]
    return lax.ppermute(value, axis, pairs)


def along_x(part, offset):
    return shifted(part, "gx", offset)


def along_y(part, offset):
    return shifted(part, "gy", offset)


def face_sum(local):
    width = local.shape[0] // 4
    low_x = local[0:width]
    high_x = local[width : 2 * width]
    low_y = local[2 * width : 3 * width]
    high_y = local[3 * width : 4 * width]
    return jnp.concatenate(
        [
            low_x + along_x(high_x, 1),
            high_x + along_x(low_x, -1),
            low_y + along_y(high_y, 1),
            high_y + along_y(low_y, -1),
        ],
        axis=0,
    )


def swap_pairs(count, first):
    pairs = []
    for low in range(first, count - 1, 2):
        pairs += [(low, low + 1), (low + 1, low)]
    return pairs


def axis_exchange(low, high, axis):
    count = lax.axis_size(axis)
    even = lax.axis_index(axis) % 2 == 0
    odd_recv = lax.ppermute(jnp.where(even, low, high), axis, swap_pairs(count, 1))
    even_recv = lax.ppermute(jnp.where(even, high, low), axis, swap_pairs(count, 0))
    new_low = low + jnp.where(even, odd_recv, even_recv)
    new_high = high + jnp.where(even, even_recv, odd_recv)
    return new_low, new_high


def face_sum_parts(faces):
    low_x, high_x, low_y, high_y = faces
    new_low_y, new_high_y = axis_exchange(low_y, high_y, "gy")
    new_low_x, new_high_x = axis_exchange(low_x, high_x, "gx")
    return jnp.concatenate([new_low_x, new_high_x, new_low_y, new_high_y], axis=0)


def exact_select(pick, values):
    high = lax.reduce_precision(values, exponent_bits=8, mantissa_bits=7)
    rest = values - high
    mid = lax.reduce_precision(rest, exponent_bits=8, mantissa_bits=7)
    low = rest - mid
    parts = [
        jnp.dot(pick, piece.astype(jnp.bfloat16), preferred_element_type=jnp.float32)
        for piece in (high, mid, low)
    ]
    return (parts[0] + parts[1]) + parts[2]


def body(gap, own_rows, spill_rows, tile_plan, orders, slot_rows):
    order_max = gap.shape[2]
    tile_rows = spill_rows.shape[3]
    own_tiles = own_rows.shape[2] // tile_rows
    hop_span = lax.axis_size("gx") // 4
    own_block = own_rows[0, 0]
    spill_block = spill_rows[0, 0]
    plan_row = tile_plan[0, 0]
    order_now = orders[0, 0]
    slot_map = slot_rows[0, 0]
    row_ids = jnp.arange(order_max, dtype=jnp.int32)
    face_sign = jnp.where(row_ids // (order_max // 4) % 2 == 0, -1.0, 1.0).astype(jnp.float32)
    slot_scale = face_sign * (slot_map < order_now).astype(jnp.float32)
    homed = [
        from_behind(spill_block[slot_id], "gx", -(slot_id + 1) * hop_span) for slot_id in range(2)
    ]
    own_count = own_block.shape[0]
    width = order_max // 4
    load = face_sum_parts([gap[0, 0, face_id * width : (face_id + 1) * width] for face_id in range(4)])
    to_slots = jnp.where(
        slot_map[:, None] == row_ids[None, :], slot_scale[:, None], 0.0
    ).astype(jnp.bfloat16)
    to_rows = jnp.where(
        row_ids[:, None] == slot_map[None, :], slot_scale[None, :], 0.0
    ).astype(jnp.bfloat16)
    extra_rows = []
    for extra_id in range(2):
        gathered = jnp.zeros_like(homed[0])
        for slot_id in range(2):
            gathered = gathered + jnp.where(
                plan_row[slot_id] == own_tiles + extra_id, homed[slot_id], 0.0
            )
        extra_rows.append(gathered)
    extra_block = jnp.concatenate(extra_rows, axis=0)
    centre = (high_bound + low_bound) / 2.0
    half_width = (high_bound - low_bound) / 2.0
    sigma_value = centre / half_width
    rho_value = 1.0 / sigma_value
    solution = jnp.zeros_like(load)
    residual = load
    direction = residual / centre
    for step_id in range(ITERS):
        solution = solution + direction
        multipliers = exact_select(to_rows, direction)
        own_out = jnp.dot(
            own_block, multipliers, precision=lax.Precision.HIGH, preferred_element_type=jnp.float32
        )
        extra_out = jnp.dot(
            extra_block, multipliers, precision=lax.Precision.HIGH, preferred_element_type=jnp.float32
        )
        faces = [
            exact_select(to_slots[face_id * width : (face_id + 1) * width, :own_count], own_out)
            + exact_select(to_slots[face_id * width : (face_id + 1) * width, own_count:], extra_out)
            for face_id in range(4)
        ]
        residual = residual - face_sum_parts(faces)
        if step_id + 1 < ITERS:
            rho_next = 1.0 / (2.0 * sigma_value - rho_value)
            direction = rho_next * rho_value * direction + 2.0 * rho_next / half_width * residual
            rho_value = rho_next
    return (solution[None, None], residual[None, None])


def solution(mesh):
    in_specs = (
        P("gx", "gy", None, None),
        P("gx", "gy", None, None),
        P("gx", "gy", None, None, None),
        P("gx", "gy", None),
        P("gx", "gy"),
        P("gx", "gy", None),
    )
    out_specs = (P("gx", "gy", None, None), P("gx", "gy", None, None))
    return jax.shard_map(body, mesh=mesh, in_specs=in_specs, out_specs=out_specs, check_vma=False)
```

```python
import jax
import jax.numpy as jnp
from jax import lax
from jax.sharding import PartitionSpec as P

ITERS = 4


low_bound = 0.5
high_bound = 7.0


def shifted(block, axis, distance):
    devices = range(lax.axis_size(axis))
    route = [(i - distance, i) for i in devices if i - distance in devices]
    return lax.ppermute(block, axis, route)


def from_behind(value, axis, steps):
    count = lax.axis_size(axis)
    pairs = [(source, (source + steps) % count) for source in range(count)]
    return lax.ppermute(value, axis, pairs)


def along_x(part, offset):
    return shifted(part, "gx", offset)


def along_y(part, offset):
    return shifted(part, "gy", offset)


def face_sum(local):
    width = local.shape[0] // 4
    low_x = local[0:width]
    high_x = local[width : 2 * width]
    low_y = local[2 * width : 3 * width]
    high_y = local[3 * width : 4 * width]
    return jnp.concatenate(
        [
            low_x + along_x(high_x, 1),
            high_x + along_x(low_x, -1),
            low_y + along_y(high_y, 1),
            high_y + along_y(low_y, -1),
        ],
        axis=0,
    )


def swap_pairs(count, first):
    pairs = []
    for low in range(first, count - 1, 2):
        pairs += [(low, low + 1), (low + 1, low)]
    return pairs


def axis_exchange(low, high, axis):
    count = lax.axis_size(axis)
    even = lax.axis_index(axis) % 2 == 0
    odd_recv = lax.ppermute(jnp.where(even, low, high), axis, swap_pairs(count, 1))
    even_recv = lax.ppermute(jnp.where(even, high, low), axis, swap_pairs(count, 0))
    new_low = low + jnp.where(even, odd_recv, even_recv)
    new_high = high + jnp.where(even, even_recv, odd_recv)
    return new_low, new_high


def face_sum_parts(faces):
    low_x, high_x, low_y, high_y = faces
    new_low_y, new_high_y = axis_exchange(low_y, high_y, "gy")
    new_low_x, new_high_x = axis_exchange(low_x, high_x, "gx")
    return jnp.concatenate([new_low_x, new_high_x, new_low_y, new_high_y], axis=0)


def slot_pieces(rows, to_rows, to_slots):
    high = lax.reduce_precision(rows, exponent_bits=8, mantissa_bits=7)
    mid = lax.reduce_precision(rows - high, exponent_bits=8, mantissa_bits=7)
    count = rows.shape[0]
    stacked = jnp.concatenate([high, mid], axis=0).astype(jnp.bfloat16)
    by_cols = jnp.dot(stacked, to_rows, preferred_element_type=jnp.float32).astype(jnp.bfloat16)
    side = jnp.concatenate([by_cols[:count], by_cols[count:]], axis=1)
    return jnp.dot(to_slots, side, preferred_element_type=jnp.float32)


def body(gap, own_rows, spill_rows, tile_plan, orders, slot_rows):
    order_max = gap.shape[2]
    tile_rows = spill_rows.shape[3]
    own_tiles = own_rows.shape[2] // tile_rows
    hop_span = lax.axis_size("gx") // 4
    own_block = own_rows[0, 0]
    spill_block = spill_rows[0, 0]
    plan_row = tile_plan[0, 0]
    order_now = orders[0, 0]
    slot_map = slot_rows[0, 0]
    row_ids = jnp.arange(order_max, dtype=jnp.int32)
    face_sign = jnp.where(row_ids // (order_max // 4) % 2 == 0, -1.0, 1.0).astype(jnp.float32)
    slot_scale = face_sign * (slot_map < order_now).astype(jnp.float32)
    homed = [
        from_behind(spill_block[slot_id], "gx", -(slot_id + 1) * hop_span) for slot_id in range(2)
    ]
    own_count = own_block.shape[0]
    cols = gap.shape[3]
    width = order_max // 4
    load = face_sum_parts([gap[0, 0, face_id * width : (face_id + 1) * width] for face_id in range(4)])
    to_slots = jnp.where(
        slot_map[:, None] == row_ids[None, :], slot_scale[:, None], 0.0
    ).astype(jnp.bfloat16)
    to_rows = jnp.where(
        row_ids[:, None] == slot_map[None, :], slot_scale[None, :], 0.0
    ).astype(jnp.bfloat16)
    own_slots = slot_pieces(own_block, to_rows, to_slots[:, :own_count])
    extra_rows = []
    for extra_id in range(2):
        gathered = jnp.zeros_like(homed[0])
        for slot_id in range(2):
            gathered = gathered + jnp.where(
                plan_row[slot_id] == own_tiles + extra_id, homed[slot_id], 0.0
            )
        extra_rows.append(gathered)
    extra_block = jnp.concatenate(extra_rows, axis=0)
    extra_slots = slot_pieces(extra_block, to_rows, to_slots[:, own_count:])
    op_high = (own_slots[:, :order_max] + extra_slots[:, :order_max]).astype(jnp.bfloat16)
    op_mid = (own_slots[:, order_max:] + extra_slots[:, order_max:]).astype(jnp.bfloat16)
    centre = (high_bound + low_bound) / 2.0
    half_width = (high_bound - low_bound) / 2.0
    sigma_value = centre / half_width
    rho_value = 1.0 / sigma_value
    solution = jnp.zeros_like(load)
    residual = load
    direction = residual / centre
    for step_id in range(ITERS):
        solution = solution + direction
        dir_high = lax.reduce_precision(direction, exponent_bits=8, mantissa_bits=7)
        dir_mid = direction - dir_high
        both = jnp.dot(
            op_high,
            jnp.concatenate([dir_high, dir_mid], axis=1).astype(jnp.bfloat16),
            preferred_element_type=jnp.float32,
        )
        local = (both[:, :cols] + both[:, cols:]) + jnp.dot(
            op_mid, dir_high.astype(jnp.bfloat16), preferred_element_type=jnp.float32
        )
        faces = [local[face_id * width : (face_id + 1) * width] for face_id in range(4)]
        residual = residual - face_sum_parts(faces)
        if step_id + 1 < ITERS:
            rho_next = 1.0 / (2.0 * sigma_value - rho_value)
            direction = rho_next * rho_value * direction + 2.0 * rho_next / half_width * residual
            rho_value = rho_next
    return (solution[None, None], residual[None, None])


def solution(mesh):
    in_specs = (
        P("gx", "gy", None, None),
        P("gx", "gy", None, None),
        P("gx", "gy", None, None, None),
        P("gx", "gy", None),
        P("gx", "gy"),
        P("gx", "gy", None),
    )
    out_specs = (P("gx", "gy", None, None), P("gx", "gy", None, None))
    return jax.shard_map(body, mesh=mesh, in_specs=in_specs, out_specs=out_specs, check_vma=False)
```

```python
import jax
import jax.numpy as jnp
from jax import lax
from jax.sharding import PartitionSpec as P

ITERS = 4


low_bound = 0.5
high_bound = 7.0


def shifted(block, axis, distance):
    devices = range(lax.axis_size(axis))
    route = [(i - distance, i) for i in devices if i - distance in devices]
    return lax.ppermute(block, axis, route)


def from_behind(value, axis, steps):
    count = lax.axis_size(axis)
    pairs = [(source, (source + steps) % count) for source in range(count)]
    return lax.ppermute(value, axis, pairs)


def along_x(part, offset):
    return shifted(part, "gx", offset)


def along_y(part, offset):
    return shifted(part, "gy", offset)


def face_sum(local):
    width = local.shape[0] // 4
    low_x = local[0:width]
    high_x = local[width : 2 * width]
    low_y = local[2 * width : 3 * width]
    high_y = local[3 * width : 4 * width]
    return jnp.concatenate(
        [
            low_x + along_x(high_x, 1),
            high_x + along_x(low_x, -1),
            low_y + along_y(high_y, 1),
            high_y + along_y(low_y, -1),
        ],
        axis=0,
    )


def swap_pairs(count, first):
    pairs = []
    for low in range(first, count - 1, 2):
        pairs += [(low, low + 1), (low + 1, low)]
    return pairs


def face_sum_parts(faces):
    low_x, high_x, low_y, high_y = faces
    sides = [(low_y, high_y, "gy"), (low_x, high_x, "gx")]
    sends = []
    for low, high, axis in sides:
        even = lax.axis_index(axis) % 2 == 0
        sends.append((jnp.where(even, low, high), swap_pairs(lax.axis_size(axis), 1), axis))
        sends.append((jnp.where(even, high, low), swap_pairs(lax.axis_size(axis), 0), axis))
    received = lax.optimization_barrier(
        [lax.ppermute(block, axis, pairs) for block, pairs, axis in sends]
    )
    summed = []
    for side_id, (low, high, axis) in enumerate(sides):
        even = lax.axis_index(axis) % 2 == 0
        odd_recv, even_recv = received[2 * side_id], received[2 * side_id + 1]
        summed.append(low + jnp.where(even, odd_recv, even_recv))
        summed.append(high + jnp.where(even, even_recv, odd_recv))
    new_low_y, new_high_y, new_low_x, new_high_x = summed
    return jnp.concatenate([new_low_x, new_high_x, new_low_y, new_high_y], axis=0)


def slot_pieces(rows, to_rows, to_slots):
    high = lax.reduce_precision(rows, exponent_bits=8, mantissa_bits=7)
    mid = lax.reduce_precision(rows - high, exponent_bits=8, mantissa_bits=7)
    count = rows.shape[0]
    stacked = jnp.concatenate([high, mid], axis=0).astype(jnp.bfloat16)
    by_cols = jnp.dot(stacked, to_rows, preferred_element_type=jnp.float32).astype(jnp.bfloat16)
    side = jnp.concatenate([by_cols[:count], by_cols[count:]], axis=1)
    return jnp.dot(to_slots, side, preferred_element_type=jnp.float32)


def body(gap, own_rows, spill_rows, tile_plan, orders, slot_rows):
    order_max = gap.shape[2]
    tile_rows = spill_rows.shape[3]
    own_tiles = own_rows.shape[2] // tile_rows
    hop_span = lax.axis_size("gx") // 4
    own_block = own_rows[0, 0]
    spill_block = spill_rows[0, 0]
    plan_row = tile_plan[0, 0]
    order_now = orders[0, 0]
    slot_map = slot_rows[0, 0]
    row_ids = jnp.arange(order_max, dtype=jnp.int32)
    face_sign = jnp.where(row_ids // (order_max // 4) % 2 == 0, -1.0, 1.0).astype(jnp.float32)
    slot_scale = face_sign * (slot_map < order_now).astype(jnp.float32)
    homed = [
        from_behind(spill_block[slot_id], "gx", -(slot_id + 1) * hop_span) for slot_id in range(2)
    ]
    own_count = own_block.shape[0]
    cols = gap.shape[3]
    width = order_max // 4
    load = face_sum_parts([gap[0, 0, face_id * width : (face_id + 1) * width] for face_id in range(4)])
    to_slots = jnp.where(
        slot_map[:, None] == row_ids[None, :], slot_scale[:, None], 0.0
    ).astype(jnp.bfloat16)
    to_rows = jnp.where(
        row_ids[:, None] == slot_map[None, :], slot_scale[None, :], 0.0
    ).astype(jnp.bfloat16)
    own_slots = slot_pieces(own_block, to_rows, to_slots[:, :own_count])
    extra_rows = []
    for extra_id in range(2):
        gathered = jnp.zeros_like(homed[0])
        for slot_id in range(2):
            gathered = gathered + jnp.where(
                plan_row[slot_id] == own_tiles + extra_id, homed[slot_id], 0.0
            )
        extra_rows.append(gathered)
    extra_block = jnp.concatenate(extra_rows, axis=0)
    extra_slots = slot_pieces(extra_block, to_rows, to_slots[:, own_count:])
    op_high = (own_slots[:, :order_max] + extra_slots[:, :order_max]).astype(jnp.bfloat16)
    op_mid = (own_slots[:, order_max:] + extra_slots[:, order_max:]).astype(jnp.bfloat16)
    centre = (high_bound + low_bound) / 2.0
    half_width = (high_bound - low_bound) / 2.0
    sigma_value = centre / half_width
    rho_value = 1.0 / sigma_value
    solution = jnp.zeros_like(load)
    residual = load
    direction = residual / centre
    for step_id in range(ITERS):
        solution = solution + direction
        dir_high = lax.reduce_precision(direction, exponent_bits=8, mantissa_bits=7)
        dir_mid = direction - dir_high
        both = jnp.dot(
            op_high,
            jnp.concatenate([dir_high, dir_mid], axis=1).astype(jnp.bfloat16),
            preferred_element_type=jnp.float32,
        )
        local = (both[:, :cols] + both[:, cols:]) + jnp.dot(
            op_mid, dir_high.astype(jnp.bfloat16), preferred_element_type=jnp.float32
        )
        faces = [local[face_id * width : (face_id + 1) * width] for face_id in range(4)]
        residual = residual - face_sum_parts(faces)
        if step_id + 1 < ITERS:
            rho_next = 1.0 / (2.0 * sigma_value - rho_value)
            direction = rho_next * rho_value * direction + 2.0 * rho_next / half_width * residual
            rho_value = rho_next
    return (solution[None, None], residual[None, None])


def solution(mesh):
    in_specs = (
        P("gx", "gy", None, None),
        P("gx", "gy", None, None),
        P("gx", "gy", None, None, None),
        P("gx", "gy", None),
        P("gx", "gy"),
        P("gx", "gy", None),
    )
    out_specs = (P("gx", "gy", None, None), P("gx", "gy", None, None))
    return jax.shard_map(body, mesh=mesh, in_specs=in_specs, out_specs=out_specs, check_vma=False)
```

```python
import jax
import jax.numpy as jnp
from jax import lax
from jax.sharding import PartitionSpec as P

ITERS = 4


low_bound = 0.5
high_bound = 7.0


def shifted(block, axis, distance):
    devices = range(lax.axis_size(axis))
    route = [(i - distance, i) for i in devices if i - distance in devices]
    return lax.ppermute(block, axis, route)


def from_behind(value, axis, steps):
    count = lax.axis_size(axis)
    pairs = [(source, (source + steps) % count) for source in range(count)]
    return lax.ppermute(value, axis, pairs)


def along_x(part, offset):
    return shifted(part, "gx", offset)


def along_y(part, offset):
    return shifted(part, "gy", offset)


def face_sum(local):
    width = local.shape[0] // 4
    low_x = local[0:width]
    high_x = local[width : 2 * width]
    low_y = local[2 * width : 3 * width]
    high_y = local[3 * width : 4 * width]
    return jnp.concatenate(
        [
            low_x + along_x(high_x, 1),
            high_x + along_x(low_x, -1),
            low_y + along_y(high_y, 1),
            high_y + along_y(low_y, -1),
        ],
        axis=0,
    )


def swap_pairs(count, first):
    pairs = []
    for low in range(first, count - 1, 2):
        pairs += [(low, low + 1), (low + 1, low)]
    return pairs


def face_sum_parts(faces, one_axis_at_a_time=False):
    low_x, high_x, low_y, high_y = faces
    sides = [(low_y, high_y, "gy"), (low_x, high_x, "gx")]
    sends = []
    for low, high, axis in sides:
        even = lax.axis_index(axis) % 2 == 0
        sends.append((jnp.where(even, low, high), swap_pairs(lax.axis_size(axis), 1), axis))
        sends.append((jnp.where(even, high, low), swap_pairs(lax.axis_size(axis), 0), axis))
    if one_axis_at_a_time:
        first = [lax.ppermute(block, axis, pairs) for block, pairs, axis in sends[:2]]
        later, first = lax.optimization_barrier(([block for block, _, _ in sends[2:]], first))
        second = [
            lax.ppermute(block, axis, pairs)
            for block, (_, pairs, axis) in zip(later, sends[2:])
        ]
        received = lax.optimization_barrier(first + second)
    else:
        received = lax.optimization_barrier(
            [lax.ppermute(block, axis, pairs) for block, pairs, axis in sends]
        )
    summed = []
    for side_id, (low, high, axis) in enumerate(sides):
        even = lax.axis_index(axis) % 2 == 0
        odd_recv, even_recv = received[2 * side_id], received[2 * side_id + 1]
        summed.append(low + jnp.where(even, odd_recv, even_recv))
        summed.append(high + jnp.where(even, even_recv, odd_recv))
    new_low_y, new_high_y, new_low_x, new_high_x = summed
    return jnp.concatenate([new_low_x, new_high_x, new_low_y, new_high_y], axis=0)


def slot_pieces(rows, to_rows, to_slots):
    high = lax.reduce_precision(rows, exponent_bits=8, mantissa_bits=7)
    mid = lax.reduce_precision(rows - high, exponent_bits=8, mantissa_bits=7)
    count = rows.shape[0]
    stacked = jnp.concatenate([high, mid], axis=0).astype(jnp.bfloat16)
    by_cols = jnp.dot(stacked, to_rows, preferred_element_type=jnp.float32).astype(jnp.bfloat16)
    side = jnp.concatenate([by_cols[:count], by_cols[count:]], axis=1)
    return jnp.dot(to_slots, side, preferred_element_type=jnp.float32)


def body(gap, own_rows, spill_rows, tile_plan, orders, slot_rows):
    order_max = gap.shape[2]
    tile_rows = spill_rows.shape[3]
    own_tiles = own_rows.shape[2] // tile_rows
    hop_span = lax.axis_size("gx") // 4
    own_block = own_rows[0, 0]
    spill_block = spill_rows[0, 0]
    plan_row = tile_plan[0, 0]
    order_now = orders[0, 0]
    slot_map = slot_rows[0, 0]
    row_ids = jnp.arange(order_max, dtype=jnp.int32)
    face_sign = jnp.where(row_ids // (order_max // 4) % 2 == 0, -1.0, 1.0).astype(jnp.float32)
    slot_scale = face_sign * (slot_map < order_now).astype(jnp.float32)
    homed = [
        from_behind(spill_block[slot_id], "gx", -(slot_id + 1) * hop_span) for slot_id in range(2)
    ]
    own_count = own_block.shape[0]
    cols = gap.shape[3]
    width = order_max // 4
    load = face_sum_parts(
        [gap[0, 0, face_id * width : (face_id + 1) * width] for face_id in range(4)],
        one_axis_at_a_time=True,
    )
    to_slots = jnp.where(
        slot_map[:, None] == row_ids[None, :], slot_scale[:, None], 0.0
    ).astype(jnp.bfloat16)
    to_rows = jnp.where(
        row_ids[:, None] == slot_map[None, :], slot_scale[None, :], 0.0
    ).astype(jnp.bfloat16)
    own_slots = slot_pieces(own_block, to_rows, to_slots[:, :own_count])
    extra_rows = []
    for extra_id in range(2):
        gathered = jnp.zeros_like(homed[0])
        for slot_id in range(2):
            gathered = gathered + jnp.where(
                plan_row[slot_id] == own_tiles + extra_id, homed[slot_id], 0.0
            )
        extra_rows.append(gathered)
    extra_block = jnp.concatenate(extra_rows, axis=0)
    extra_slots = slot_pieces(extra_block, to_rows, to_slots[:, own_count:])
    op_high = (own_slots[:, :order_max] + extra_slots[:, :order_max]).astype(jnp.bfloat16)
    op_mid = (own_slots[:, order_max:] + extra_slots[:, order_max:]).astype(jnp.bfloat16)
    centre = (high_bound + low_bound) / 2.0
    half_width = (high_bound - low_bound) / 2.0
    sigma_value = centre / half_width
    rho_value = 1.0 / sigma_value
    solution = jnp.zeros_like(load)
    residual = load
    direction = residual / centre
    for step_id in range(ITERS):
        solution = solution + direction
        dir_high = lax.reduce_precision(direction, exponent_bits=8, mantissa_bits=7)
        dir_mid = direction - dir_high
        both = jnp.dot(
            op_high,
            jnp.concatenate([dir_high, dir_mid], axis=1).astype(jnp.bfloat16),
            preferred_element_type=jnp.float32,
        )
        local = (both[:, :cols] + both[:, cols:]) + jnp.dot(
            op_mid, dir_high.astype(jnp.bfloat16), preferred_element_type=jnp.float32
        )
        faces = [local[face_id * width : (face_id + 1) * width] for face_id in range(4)]
        residual = residual - face_sum_parts(faces)
        if step_id + 1 < ITERS:
            rho_next = 1.0 / (2.0 * sigma_value - rho_value)
            direction = rho_next * rho_value * direction + 2.0 * rho_next / half_width * residual
            rho_value = rho_next
    return (solution[None, None], residual[None, None])


def solution(mesh):
    in_specs = (
        P("gx", "gy", None, None),
        P("gx", "gy", None, None),
        P("gx", "gy", None, None, None),
        P("gx", "gy", None),
        P("gx", "gy"),
        P("gx", "gy", None),
    )
    out_specs = (P("gx", "gy", None, None), P("gx", "gy", None, None))
    return jax.shard_map(body, mesh=mesh, in_specs=in_specs, out_specs=out_specs, check_vma=False)
```

```python
import jax
import jax.numpy as jnp
from jax import lax
from jax.sharding import PartitionSpec as P

ITERS = 4


low_bound = 0.5
high_bound = 7.0


def shifted(block, axis, distance):
    devices = range(lax.axis_size(axis))
    route = [(i - distance, i) for i in devices if i - distance in devices]
    return lax.ppermute(block, axis, route)


def from_behind(value, axis, steps):
    count = lax.axis_size(axis)
    pairs = [(source, (source + steps) % count) for source in range(count)]
    return lax.ppermute(value, axis, pairs)


def along_x(part, offset):
    return shifted(part, "gx", offset)


def along_y(part, offset):
    return shifted(part, "gy", offset)


def face_sum(local):
    width = local.shape[0] // 4
    low_x = local[0:width]
    high_x = local[width : 2 * width]
    low_y = local[2 * width : 3 * width]
    high_y = local[3 * width : 4 * width]
    return jnp.concatenate(
        [
            low_x + along_x(high_x, 1),
            high_x + along_x(low_x, -1),
            low_y + along_y(high_y, 1),
            high_y + along_y(low_y, -1),
        ],
        axis=0,
    )


def swap_pairs(count, first):
    pairs = []
    for low in range(first, count - 1, 2):
        pairs += [(low, low + 1), (low + 1, low)]
    return pairs


def face_sum_parts(faces, one_axis_at_a_time=False):
    low_x, high_x, low_y, high_y = faces
    sides = [(low_y, high_y, "gy"), (low_x, high_x, "gx")]
    sends = []
    for low, high, axis in sides:
        even = lax.axis_index(axis) % 2 == 0
        sends.append((jnp.where(even, low, high), swap_pairs(lax.axis_size(axis), 1), axis))
        sends.append((jnp.where(even, high, low), swap_pairs(lax.axis_size(axis), 0), axis))
    if one_axis_at_a_time:
        first = [lax.ppermute(block, axis, pairs) for block, pairs, axis in sends[:2]]
        later, first = lax.optimization_barrier(([block for block, _, _ in sends[2:]], first))
        second = [
            lax.ppermute(block, axis, pairs)
            for block, (_, pairs, axis) in zip(later, sends[2:])
        ]
        received = lax.optimization_barrier(first + second)
    else:
        received = lax.optimization_barrier(
            [lax.ppermute(block, axis, pairs) for block, pairs, axis in sends]
        )
    summed = []
    for side_id, (low, high, axis) in enumerate(sides):
        even = lax.axis_index(axis) % 2 == 0
        odd_recv, even_recv = received[2 * side_id], received[2 * side_id + 1]
        summed.append(low + jnp.where(even, odd_recv, even_recv))
        summed.append(high + jnp.where(even, even_recv, odd_recv))
    new_low_y, new_high_y, new_low_x, new_high_x = summed
    return jnp.concatenate([new_low_x, new_high_x, new_low_y, new_high_y], axis=0)


def slot_pieces(rows, to_rows, to_slots):
    high = lax.reduce_precision(rows, exponent_bits=8, mantissa_bits=7)
    mid = lax.reduce_precision(rows - high, exponent_bits=8, mantissa_bits=7)
    count = rows.shape[0]
    stacked = jnp.concatenate([high, mid], axis=0).astype(jnp.bfloat16)
    by_cols = jnp.dot(stacked, to_rows, preferred_element_type=jnp.float32).astype(jnp.bfloat16)
    side = jnp.concatenate([by_cols[:count], by_cols[count:]], axis=1)
    return jnp.dot(to_slots, side, preferred_element_type=jnp.float32)


def bf16x3_apply(op_high, op_mid, pair, cols):
    both = jnp.dot(op_high, pair, preferred_element_type=jnp.float32)
    return (both[:, :cols] + both[:, cols:]) + jnp.dot(
        op_mid, pair[:, :cols], preferred_element_type=jnp.float32
    )


def body(gap, own_rows, spill_rows, tile_plan, orders, slot_rows):
    order_max = gap.shape[2]
    tile_rows = spill_rows.shape[3]
    own_tiles = own_rows.shape[2] // tile_rows
    hop_span = lax.axis_size("gx") // 4
    own_block = own_rows[0, 0]
    spill_block = spill_rows[0, 0]
    plan_row = tile_plan[0, 0]
    order_now = orders[0, 0]
    slot_map = slot_rows[0, 0]
    row_ids = jnp.arange(order_max, dtype=jnp.int32)
    face_sign = jnp.where(row_ids // (order_max // 4) % 2 == 0, -1.0, 1.0).astype(jnp.float32)
    slot_scale = face_sign * (slot_map < order_now).astype(jnp.float32)
    homed = [
        from_behind(spill_block[slot_id], "gx", -(slot_id + 1) * hop_span) for slot_id in range(2)
    ]
    own_count = own_block.shape[0]
    cols = gap.shape[3]
    width = order_max // 4
    load = face_sum_parts(
        [gap[0, 0, face_id * width : (face_id + 1) * width] for face_id in range(4)],
        one_axis_at_a_time=True,
    )
    to_slots = jnp.where(
        slot_map[:, None] == row_ids[None, :], slot_scale[:, None], 0.0
    ).astype(jnp.bfloat16)
    to_rows = jnp.where(
        row_ids[:, None] == slot_map[None, :], slot_scale[None, :], 0.0
    ).astype(jnp.bfloat16)
    own_slots = slot_pieces(own_block, to_rows, to_slots[:, :own_count])
    spill_ids = jnp.concatenate(
        [
            jnp.where(plan_row[slot_id] >= own_tiles, plan_row[slot_id] * tile_rows, -order_max)
            + jnp.arange(tile_rows, dtype=jnp.int32)
            for slot_id in range(2)
        ]
    )
    spill_place = jnp.where(
        slot_map[:, None] == spill_ids[None, :], slot_scale[:, None], 0.0
    ).astype(jnp.bfloat16)
    spill_stack = jnp.concatenate(homed, axis=0)
    spill_slots = slot_pieces(spill_stack, to_rows, spill_place)
    own_high = own_slots[:, :order_max].astype(jnp.bfloat16)
    own_mid = own_slots[:, order_max:].astype(jnp.bfloat16)
    op_high = (own_slots[:, :order_max] + spill_slots[:, :order_max]).astype(jnp.bfloat16)
    op_mid = (own_slots[:, order_max:] + spill_slots[:, order_max:]).astype(jnp.bfloat16)
    spill_high = lax.reduce_precision(spill_stack, exponent_bits=8, mantissa_bits=7)
    spill_mid = (spill_stack - spill_high).astype(jnp.bfloat16)
    spill_high = spill_high.astype(jnp.bfloat16)
    centre = (high_bound + low_bound) / 2.0
    half_width = (high_bound - low_bound) / 2.0
    sigma_value = centre / half_width
    rho_value = 1.0 / sigma_value
    solution = jnp.zeros_like(load)
    residual = load
    direction = residual / centre
    for step_id in range(ITERS):
        solution = solution + direction
        dir_high = lax.reduce_precision(direction, exponent_bits=8, mantissa_bits=7)
        dir_pair = jnp.concatenate([dir_high, direction - dir_high], axis=1).astype(jnp.bfloat16)
        if step_id == 0:
            local = bf16x3_apply(own_high, own_mid, dir_pair, cols)
            moved = jnp.dot(to_rows, dir_pair, preferred_element_type=jnp.float32).astype(
                jnp.bfloat16
            )
            spill_out = bf16x3_apply(spill_high, spill_mid, moved, cols)
            out_high = lax.reduce_precision(spill_out, exponent_bits=8, mantissa_bits=7)
            out_rest = spill_out - out_high
            out_mid = lax.reduce_precision(out_rest, exponent_bits=8, mantissa_bits=7)
            pieces = jnp.concatenate([out_high, out_mid, out_rest - out_mid], axis=1)
            placed = jnp.dot(
                spill_place, pieces.astype(jnp.bfloat16), preferred_element_type=jnp.float32
            )
            local = local + (
                (placed[:, :cols] + placed[:, cols : 2 * cols]) + placed[:, 2 * cols :]
            )
        else:
            local = bf16x3_apply(op_high, op_mid, dir_pair, cols)
        faces = [local[face_id * width : (face_id + 1) * width] for face_id in range(4)]
        residual = residual - face_sum_parts(faces)
        if step_id + 1 < ITERS:
            rho_next = 1.0 / (2.0 * sigma_value - rho_value)
            direction = rho_next * rho_value * direction + 2.0 * rho_next / half_width * residual
            rho_value = rho_next
    return (solution[None, None], residual[None, None])


def solution(mesh):
    in_specs = (
        P("gx", "gy", None, None),
        P("gx", "gy", None, None),
        P("gx", "gy", None, None, None),
        P("gx", "gy", None),
        P("gx", "gy"),
        P("gx", "gy", None),
    )
    out_specs = (P("gx", "gy", None, None), P("gx", "gy", None, None))
    return jax.shard_map(body, mesh=mesh, in_specs=in_specs, out_specs=out_specs, check_vma=False)
```

```python
import jax
import jax.numpy as jnp
from jax import lax
from jax.sharding import PartitionSpec as P

ITERS = 4


low_bound = 0.5
high_bound = 7.0


def shifted(block, axis, distance):
    devices = range(lax.axis_size(axis))
    route = [(i - distance, i) for i in devices if i - distance in devices]
    return lax.ppermute(block, axis, route)


def from_behind(value, axis, steps):
    count = lax.axis_size(axis)
    pairs = [(source, (source + steps) % count) for source in range(count)]
    return lax.ppermute(value, axis, pairs)


def along_x(part, offset):
    return shifted(part, "gx", offset)


def along_y(part, offset):
    return shifted(part, "gy", offset)


def face_sum(local):
    width = local.shape[0] // 4
    low_x = local[0:width]
    high_x = local[width : 2 * width]
    low_y = local[2 * width : 3 * width]
    high_y = local[3 * width : 4 * width]
    return jnp.concatenate(
        [
            low_x + along_x(high_x, 1),
            high_x + along_x(low_x, -1),
            low_y + along_y(high_y, 1),
            high_y + along_y(low_y, -1),
        ],
        axis=0,
    )


def swap_pairs(count, first):
    pairs = []
    for low in range(first, count - 1, 2):
        pairs += [(low, low + 1), (low + 1, low)]
    return pairs


def face_sum_parts(faces, one_axis_at_a_time=False):
    low_x, high_x, low_y, high_y = faces
    sides = [(low_y, high_y, "gy"), (low_x, high_x, "gx")]
    sends = []
    for low, high, axis in sides:
        even = lax.axis_index(axis) % 2 == 0
        sends.append((jnp.where(even, low, high), swap_pairs(lax.axis_size(axis), 1), axis))
        sends.append((jnp.where(even, high, low), swap_pairs(lax.axis_size(axis), 0), axis))
    if one_axis_at_a_time:
        first = [lax.ppermute(block, axis, pairs) for block, pairs, axis in sends[2:]]
        later, first = lax.optimization_barrier(([block for block, _, _ in sends[:2]], first))
        second = [
            lax.ppermute(block, axis, pairs)
            for block, (_, pairs, axis) in zip(later, sends[:2])
        ]
        received = lax.optimization_barrier(second + first)
    else:
        received = lax.optimization_barrier(
            [lax.ppermute(block, axis, pairs) for block, pairs, axis in sends]
        )
    summed = []
    for side_id, (low, high, axis) in enumerate(sides):
        even = lax.axis_index(axis) % 2 == 0
        odd_recv, even_recv = received[2 * side_id], received[2 * side_id + 1]
        summed.append(low + jnp.where(even, odd_recv, even_recv))
        summed.append(high + jnp.where(even, even_recv, odd_recv))
    new_low_y, new_high_y, new_low_x, new_high_x = summed
    return jnp.concatenate([new_low_x, new_high_x, new_low_y, new_high_y], axis=0)


def slot_pieces(rows, to_rows, to_slots):
    high = lax.reduce_precision(rows, exponent_bits=8, mantissa_bits=7)
    mid = lax.reduce_precision(rows - high, exponent_bits=8, mantissa_bits=7)
    count = rows.shape[0]
    stacked = jnp.concatenate([high, mid], axis=0).astype(jnp.bfloat16)
    by_cols = jnp.dot(stacked, to_rows, preferred_element_type=jnp.float32).astype(jnp.bfloat16)
    side = jnp.concatenate([by_cols[:count], by_cols[count:]], axis=1)
    return jnp.dot(to_slots, side, preferred_element_type=jnp.float32)


def bf16x3_apply(op_high, op_mid, pair, cols):
    both = jnp.dot(op_high, pair, preferred_element_type=jnp.float32)
    return (both[:, :cols] + both[:, cols:]) + jnp.dot(
        op_mid, pair[:, :cols], preferred_element_type=jnp.float32
    )


def body(gap, own_rows, spill_rows, tile_plan, orders, slot_rows):
    order_max = gap.shape[2]
    tile_rows = spill_rows.shape[3]
    own_tiles = own_rows.shape[2] // tile_rows
    hop_span = lax.axis_size("gx") // 4
    own_block = own_rows[0, 0]
    spill_block = spill_rows[0, 0]
    plan_row = tile_plan[0, 0]
    order_now = orders[0, 0]
    slot_map = slot_rows[0, 0]
    row_ids = jnp.arange(order_max, dtype=jnp.int32)
    face_sign = jnp.where(row_ids // (order_max // 4) % 2 == 0, -1.0, 1.0).astype(jnp.float32)
    slot_scale = face_sign * (slot_map < order_now).astype(jnp.float32)
    spill_parts = [spill_block[slot_id] for slot_id in range(2)]
    gap_faces, spill_parts = lax.optimization_barrier((gap[0, 0], spill_parts))
    homed = [
        from_behind(spill_parts[slot_id], "gx", -(slot_id + 1) * hop_span) for slot_id in range(2)
    ]
    own_count = own_block.shape[0]
    cols = gap.shape[3]
    width = order_max // 4
    load = face_sum_parts(
        [gap_faces[face_id * width : (face_id + 1) * width] for face_id in range(4)],
        one_axis_at_a_time=True,
    )
    to_slots = jnp.where(
        slot_map[:, None] == row_ids[None, :], slot_scale[:, None], 0.0
    ).astype(jnp.bfloat16)
    to_rows = jnp.where(
        row_ids[:, None] == slot_map[None, :], slot_scale[None, :], 0.0
    ).astype(jnp.bfloat16)
    own_slots = slot_pieces(own_block, to_rows, to_slots[:, :own_count])
    spill_ids = jnp.concatenate(
        [
            jnp.where(plan_row[slot_id] >= own_tiles, plan_row[slot_id] * tile_rows, -order_max)
            + jnp.arange(tile_rows, dtype=jnp.int32)
            for slot_id in range(2)
        ]
    )
    spill_place = jnp.where(
        slot_map[:, None] == spill_ids[None, :], slot_scale[:, None], 0.0
    ).astype(jnp.bfloat16)
    spill_stack = jnp.concatenate(homed, axis=0)
    spill_slots = slot_pieces(spill_stack, to_rows, spill_place)
    own_high = own_slots[:, :order_max].astype(jnp.bfloat16)
    own_mid = own_slots[:, order_max:].astype(jnp.bfloat16)
    op_high = (own_slots[:, :order_max] + spill_slots[:, :order_max]).astype(jnp.bfloat16)
    op_mid = (own_slots[:, order_max:] + spill_slots[:, order_max:]).astype(jnp.bfloat16)
    spill_high = lax.reduce_precision(spill_stack, exponent_bits=8, mantissa_bits=7)
    spill_mid = (spill_stack - spill_high).astype(jnp.bfloat16)
    spill_high = spill_high.astype(jnp.bfloat16)
    centre = (high_bound + low_bound) / 2.0
    half_width = (high_bound - low_bound) / 2.0
    sigma_value = centre / half_width
    rho_value = 1.0 / sigma_value
    solution = jnp.zeros_like(load)
    residual = load
    direction = residual / centre
    for step_id in range(ITERS):
        solution = solution + direction
        dir_high = lax.reduce_precision(direction, exponent_bits=8, mantissa_bits=7)
        dir_pair = jnp.concatenate([dir_high, direction - dir_high], axis=1).astype(jnp.bfloat16)
        if step_id == 0:
            local = bf16x3_apply(own_high, own_mid, dir_pair, cols)
            moved = jnp.dot(to_rows, dir_pair, preferred_element_type=jnp.float32).astype(
                jnp.bfloat16
            )
            spill_out = bf16x3_apply(spill_high, spill_mid, moved, cols)
            out_high = lax.reduce_precision(spill_out, exponent_bits=8, mantissa_bits=7)
            out_rest = spill_out - out_high
            out_mid = lax.reduce_precision(out_rest, exponent_bits=8, mantissa_bits=7)
            pieces = jnp.concatenate([out_high, out_mid, out_rest - out_mid], axis=1)
            placed = jnp.dot(
                spill_place, pieces.astype(jnp.bfloat16), preferred_element_type=jnp.float32
            )
            local = local + (
                (placed[:, :cols] + placed[:, cols : 2 * cols]) + placed[:, 2 * cols :]
            )
        else:
            local = bf16x3_apply(op_high, op_mid, dir_pair, cols)
        faces = [local[face_id * width : (face_id + 1) * width] for face_id in range(4)]
        residual = residual - face_sum_parts(faces)
        if step_id + 1 < ITERS:
            rho_next = 1.0 / (2.0 * sigma_value - rho_value)
            direction = rho_next * rho_value * direction + 2.0 * rho_next / half_width * residual
            rho_value = rho_next
    return (solution[None, None], residual[None, None])


def solution(mesh):
    in_specs = (
        P("gx", "gy", None, None),
        P("gx", "gy", None, None),
        P("gx", "gy", None, None, None),
        P("gx", "gy", None),
        P("gx", "gy"),
        P("gx", "gy", None),
    )
    out_specs = (P("gx", "gy", None, None), P("gx", "gy", None, None))
    return jax.shard_map(body, mesh=mesh, in_specs=in_specs, out_specs=out_specs, check_vma=False)
```

```python
import jax
import jax.numpy as jnp
from jax import lax
from jax.sharding import PartitionSpec as P

ITERS = 4


low_bound = 0.5
high_bound = 7.0


def shifted(block, axis, distance):
    devices = range(lax.axis_size(axis))
    route = [(i - distance, i) for i in devices if i - distance in devices]
    return lax.ppermute(block, axis, route)


def from_behind(value, axis, steps):
    count = lax.axis_size(axis)
    pairs = [(source, (source + steps) % count) for source in range(count)]
    return lax.ppermute(value, axis, pairs)


def along_x(part, offset):
    return shifted(part, "gx", offset)


def along_y(part, offset):
    return shifted(part, "gy", offset)


def face_sum(local):
    width = local.shape[0] // 4
    low_x = local[0:width]
    high_x = local[width : 2 * width]
    low_y = local[2 * width : 3 * width]
    high_y = local[3 * width : 4 * width]
    return jnp.concatenate(
        [
            low_x + along_x(high_x, 1),
            high_x + along_x(low_x, -1),
            low_y + along_y(high_y, 1),
            high_y + along_y(low_y, -1),
        ],
        axis=0,
    )


def swap_pairs(count, first):
    pairs = []
    for low in range(first, count - 1, 2):
        pairs += [(low, low + 1), (low + 1, low)]
    return pairs


def face_sum_parts(faces, one_axis_at_a_time=False):
    low_x, high_x, low_y, high_y = faces
    sides = [(low_y, high_y, "gy"), (low_x, high_x, "gx")]
    sends = []
    for low, high, axis in sides:
        even = lax.axis_index(axis) % 2 == 0
        sends.append((jnp.where(even, low, high), swap_pairs(lax.axis_size(axis), 1), axis))
        sends.append((jnp.where(even, high, low), swap_pairs(lax.axis_size(axis), 0), axis))
    if one_axis_at_a_time:
        first = [lax.ppermute(block, axis, pairs) for block, pairs, axis in sends[2:]]
        later, first = lax.optimization_barrier(([block for block, _, _ in sends[:2]], first))
        second = [
            lax.ppermute(block, axis, pairs)
            for block, (_, pairs, axis) in zip(later, sends[:2])
        ]
        received = lax.optimization_barrier(second + first)
    else:
        received = lax.optimization_barrier(
            [lax.ppermute(block, axis, pairs) for block, pairs, axis in sends]
        )
    summed = []
    for side_id, (low, high, axis) in enumerate(sides):
        even = lax.axis_index(axis) % 2 == 0
        odd_recv, even_recv = received[2 * side_id], received[2 * side_id + 1]
        summed.append(low + jnp.where(even, odd_recv, even_recv))
        summed.append(high + jnp.where(even, even_recv, odd_recv))
    new_low_y, new_high_y, new_low_x, new_high_x = summed
    return jnp.concatenate([new_low_x, new_high_x, new_low_y, new_high_y], axis=0)


def slot_pieces(rows, to_rows, to_slots):
    high = lax.reduce_precision(rows, exponent_bits=8, mantissa_bits=7)
    mid = lax.reduce_precision(rows - high, exponent_bits=8, mantissa_bits=7)
    count = rows.shape[0]
    stacked = jnp.concatenate([high, mid], axis=0).astype(jnp.bfloat16)
    by_cols = jnp.dot(stacked, to_rows, preferred_element_type=jnp.float32).astype(jnp.bfloat16)
    side = jnp.concatenate([by_cols[:count], by_cols[count:]], axis=1)
    return jnp.dot(to_slots, side, preferred_element_type=jnp.float32)


def bf16x3_apply(op_high, op_mid, pair, cols):
    both = jnp.dot(op_high, pair, preferred_element_type=jnp.float32)
    return (both[:, :cols] + both[:, cols:]) + jnp.dot(
        op_mid, pair[:, :cols], preferred_element_type=jnp.float32
    )


def body(gap, own_rows, spill_rows, tile_plan, orders, slot_rows):
    order_max = gap.shape[2]
    tile_rows = spill_rows.shape[3]
    own_tiles = own_rows.shape[2] // tile_rows
    hop_span = lax.axis_size("gx") // 4
    own_block = own_rows[0, 0]
    spill_block = spill_rows[0, 0]
    plan_row = tile_plan[0, 0]
    order_now = orders[0, 0]
    slot_map = slot_rows[0, 0]
    row_ids = jnp.arange(order_max, dtype=jnp.int32)
    face_sign = jnp.where(row_ids // (order_max // 4) % 2 == 0, -1.0, 1.0).astype(jnp.float32)
    slot_scale = face_sign * (slot_map < order_now).astype(jnp.float32)
    spill_parts = [spill_block[slot_id] for slot_id in range(2)]
    gap_faces, spill_parts = lax.optimization_barrier((gap[0, 0], spill_parts))
    homed = [
        from_behind(spill_parts[slot_id], "gx", -(slot_id + 1) * hop_span) for slot_id in range(2)
    ]
    own_count = own_block.shape[0]
    cols = gap.shape[3]
    width = order_max // 4
    load = face_sum_parts(
        [gap_faces[face_id * width : (face_id + 1) * width] for face_id in range(4)],
        one_axis_at_a_time=True,
    )
    to_slots = jnp.where(
        slot_map[:, None] == row_ids[None, :], slot_scale[:, None], 0.0
    ).astype(jnp.bfloat16)
    to_rows = jnp.where(
        row_ids[:, None] == slot_map[None, :], slot_scale[None, :], 0.0
    ).astype(jnp.bfloat16)
    own_slots = slot_pieces(own_block, to_rows, to_slots[:, :own_count])
    spill_ids = jnp.concatenate(
        [
            jnp.where(plan_row[slot_id] >= own_tiles, plan_row[slot_id] * tile_rows, -order_max)
            + jnp.arange(tile_rows, dtype=jnp.int32)
            for slot_id in range(2)
        ]
    )
    spill_place = jnp.where(
        slot_map[:, None] == spill_ids[None, :], slot_scale[:, None], 0.0
    ).astype(jnp.bfloat16)
    spill_slots = [
        slot_pieces(homed[slot_id], to_rows, spill_place[:, slot_id * tile_rows : (slot_id + 1) * tile_rows])
        for slot_id in range(2)
    ]
    own_high = own_slots[:, :order_max].astype(jnp.bfloat16)
    own_mid = own_slots[:, order_max:].astype(jnp.bfloat16)
    full_slots = own_slots + (spill_slots[0] + spill_slots[1])
    op_high = full_slots[:, :order_max].astype(jnp.bfloat16)
    op_mid = full_slots[:, order_max:].astype(jnp.bfloat16)
    spill_high = [lax.reduce_precision(block, exponent_bits=8, mantissa_bits=7) for block in homed]
    spill_mid = [(block - high).astype(jnp.bfloat16) for block, high in zip(homed, spill_high)]
    spill_high = [high.astype(jnp.bfloat16) for high in spill_high]
    centre = (high_bound + low_bound) / 2.0
    half_width = (high_bound - low_bound) / 2.0
    sigma_value = centre / half_width
    rho_value = 1.0 / sigma_value
    solution = jnp.zeros_like(load)
    residual = load
    direction = residual / centre
    for step_id in range(ITERS):
        solution = solution + direction
        dir_high = lax.reduce_precision(direction, exponent_bits=8, mantissa_bits=7)
        dir_pair = jnp.concatenate([dir_high, direction - dir_high], axis=1).astype(jnp.bfloat16)
        if step_id == 0:
            local = bf16x3_apply(own_high, own_mid, dir_pair, cols)
            moved = jnp.dot(to_rows, dir_pair, preferred_element_type=jnp.float32).astype(
                jnp.bfloat16
            )
            for slot_id in range(2):
                spill_out = bf16x3_apply(spill_high[slot_id], spill_mid[slot_id], moved, cols)
                out_high = lax.reduce_precision(spill_out, exponent_bits=8, mantissa_bits=7)
                out_rest = spill_out - out_high
                out_mid = lax.reduce_precision(out_rest, exponent_bits=8, mantissa_bits=7)
                pieces = jnp.concatenate([out_high, out_mid, out_rest - out_mid], axis=1)
                placed = jnp.dot(
                    spill_place[:, slot_id * tile_rows : (slot_id + 1) * tile_rows],
                    pieces.astype(jnp.bfloat16),
                    preferred_element_type=jnp.float32,
                )
                local = local + (
                    (placed[:, :cols] + placed[:, cols : 2 * cols]) + placed[:, 2 * cols :]
                )
        else:
            local = bf16x3_apply(op_high, op_mid, dir_pair, cols)
        faces = [local[face_id * width : (face_id + 1) * width] for face_id in range(4)]
        residual = residual - face_sum_parts(faces)
        if step_id + 1 < ITERS:
            rho_next = 1.0 / (2.0 * sigma_value - rho_value)
            direction = rho_next * rho_value * direction + 2.0 * rho_next / half_width * residual
            rho_value = rho_next
    return (solution[None, None], residual[None, None])


def solution(mesh):
    in_specs = (
        P("gx", "gy", None, None),
        P("gx", "gy", None, None),
        P("gx", "gy", None, None, None),
        P("gx", "gy", None),
        P("gx", "gy"),
        P("gx", "gy", None),
    )
    out_specs = (P("gx", "gy", None, None), P("gx", "gy", None, None))
    return jax.shard_map(body, mesh=mesh, in_specs=in_specs, out_specs=out_specs, check_vma=False)
```

```python
import jax
import jax.numpy as jnp
from jax import lax
from jax.sharding import PartitionSpec as P

ITERS = 4


low_bound = 0.5
high_bound = 7.0


def shifted(block, axis, distance):
    devices = range(lax.axis_size(axis))
    route = [(i - distance, i) for i in devices if i - distance in devices]
    return lax.ppermute(block, axis, route)


def from_behind(value, axis, steps):
    count = lax.axis_size(axis)
    pairs = [(source, (source + steps) % count) for source in range(count)]
    return lax.ppermute(value, axis, pairs)


def along_x(part, offset):
    return shifted(part, "gx", offset)


def along_y(part, offset):
    return shifted(part, "gy", offset)


def face_sum(local):
    width = local.shape[0] // 4
    low_x = local[0:width]
    high_x = local[width : 2 * width]
    low_y = local[2 * width : 3 * width]
    high_y = local[3 * width : 4 * width]
    return jnp.concatenate(
        [
            low_x + along_x(high_x, 1),
            high_x + along_x(low_x, -1),
            low_y + along_y(high_y, 1),
            high_y + along_y(low_y, -1),
        ],
        axis=0,
    )


def swap_pairs(count, first):
    pairs = []
    for low in range(first, count - 1, 2):
        pairs += [(low, low + 1), (low + 1, low)]
    return pairs


def face_sum_parts(faces, one_axis_at_a_time=False):
    low_x, high_x, low_y, high_y = faces
    sides = [(low_y, high_y, "gy"), (low_x, high_x, "gx")]
    sends = []
    for low, high, axis in sides:
        even = lax.axis_index(axis) % 2 == 0
        sends.append((jnp.where(even, low, high), swap_pairs(lax.axis_size(axis), 1), axis))
        sends.append((jnp.where(even, high, low), swap_pairs(lax.axis_size(axis), 0), axis))
    if one_axis_at_a_time:
        first = [lax.ppermute(block, axis, pairs) for block, pairs, axis in sends[2:]]
        later, first = lax.optimization_barrier(([block for block, _, _ in sends[:2]], first))
        second = [
            lax.ppermute(block, axis, pairs)
            for block, (_, pairs, axis) in zip(later, sends[:2])
        ]
        received = lax.optimization_barrier(second + first)
    else:
        received = lax.optimization_barrier(
            [lax.ppermute(block, axis, pairs) for block, pairs, axis in sends]
        )
    summed = []
    for side_id, (low, high, axis) in enumerate(sides):
        even = lax.axis_index(axis) % 2 == 0
        odd_recv, even_recv = received[2 * side_id], received[2 * side_id + 1]
        summed.append(low + jnp.where(even, odd_recv, even_recv))
        summed.append(high + jnp.where(even, even_recv, odd_recv))
    new_low_y, new_high_y, new_low_x, new_high_x = summed
    return jnp.concatenate([new_low_x, new_high_x, new_low_y, new_high_y], axis=0)


def slot_pieces(rows, to_rows, to_slots):
    high = lax.reduce_precision(rows, exponent_bits=8, mantissa_bits=7)
    mid = lax.reduce_precision(rows - high, exponent_bits=8, mantissa_bits=7)
    count = rows.shape[0]
    stacked = jnp.concatenate([high, mid], axis=0).astype(jnp.bfloat16)
    by_cols = jnp.dot(stacked, to_rows, preferred_element_type=jnp.float32).astype(jnp.bfloat16)
    side = jnp.concatenate([by_cols[:count], by_cols[count:]], axis=1)
    return jnp.dot(to_slots, side, preferred_element_type=jnp.float32)


def bf16x3_apply(op_high, op_mid, pair, cols):
    both = jnp.dot(op_high, pair, preferred_element_type=jnp.float32)
    return (both[:, :cols] + both[:, cols:]) + jnp.dot(
        op_mid, pair[:, :cols], preferred_element_type=jnp.float32
    )


def body(gap, own_rows, spill_rows, tile_plan, orders, slot_rows):
    order_max = gap.shape[2]
    tile_rows = spill_rows.shape[3]
    own_tiles = own_rows.shape[2] // tile_rows
    hop_span = lax.axis_size("gx") // 4
    own_block = own_rows[0, 0]
    spill_block = spill_rows[0, 0]
    plan_row = tile_plan[0, 0]
    order_now = orders[0, 0]
    slot_map = slot_rows[0, 0]
    row_ids = jnp.arange(order_max, dtype=jnp.int32)
    face_sign = jnp.where(row_ids // (order_max // 4) % 2 == 0, -1.0, 1.0).astype(jnp.float32)
    slot_scale = face_sign * (slot_map < order_now).astype(jnp.float32)
    spill_parts = lax.optimization_barrier([spill_block[slot_id] for slot_id in range(2)])
    homed = [
        from_behind(spill_parts[slot_id], "gx", -(slot_id + 1) * hop_span) for slot_id in range(2)
    ]
    gap_faces, _ = lax.optimization_barrier((gap[0, 0], spill_parts))
    own_count = own_block.shape[0]
    cols = gap.shape[3]
    width = order_max // 4
    load = face_sum_parts(
        [gap_faces[face_id * width : (face_id + 1) * width] for face_id in range(4)],
        one_axis_at_a_time=True,
    )
    to_slots = jnp.where(
        slot_map[:, None] == row_ids[None, :], slot_scale[:, None], 0.0
    ).astype(jnp.bfloat16)
    to_rows = jnp.where(
        row_ids[:, None] == slot_map[None, :], slot_scale[None, :], 0.0
    ).astype(jnp.bfloat16)
    own_slots = slot_pieces(own_block, to_rows, to_slots[:, :own_count])
    spill_ids = jnp.concatenate(
        [
            jnp.where(plan_row[slot_id] >= own_tiles, plan_row[slot_id] * tile_rows, -order_max)
            + jnp.arange(tile_rows, dtype=jnp.int32)
            for slot_id in range(2)
        ]
    )
    spill_place = jnp.where(
        slot_map[:, None] == spill_ids[None, :], slot_scale[:, None], 0.0
    ).astype(jnp.bfloat16)
    spill_slots = [
        slot_pieces(homed[slot_id], to_rows, spill_place[:, slot_id * tile_rows : (slot_id + 1) * tile_rows])
        for slot_id in range(2)
    ]
    own_high = own_slots[:, :order_max].astype(jnp.bfloat16)
    own_mid = own_slots[:, order_max:].astype(jnp.bfloat16)
    full_slots = own_slots + (spill_slots[0] + spill_slots[1])
    op_high = full_slots[:, :order_max].astype(jnp.bfloat16)
    op_mid = full_slots[:, order_max:].astype(jnp.bfloat16)
    spill_high = [lax.reduce_precision(block, exponent_bits=8, mantissa_bits=7) for block in homed]
    spill_mid = [(block - high).astype(jnp.bfloat16) for block, high in zip(homed, spill_high)]
    spill_high = [high.astype(jnp.bfloat16) for high in spill_high]
    centre = (high_bound + low_bound) / 2.0
    half_width = (high_bound - low_bound) / 2.0
    sigma_value = centre / half_width
    rho_value = 1.0 / sigma_value
    solution = jnp.zeros_like(load)
    residual = load
    direction = residual / centre
    for step_id in range(ITERS):
        solution = solution + direction
        dir_high = lax.reduce_precision(direction, exponent_bits=8, mantissa_bits=7)
        dir_pair = jnp.concatenate([dir_high, direction - dir_high], axis=1).astype(jnp.bfloat16)
        if step_id == 0:
            local = bf16x3_apply(own_high, own_mid, dir_pair, cols)
            moved = jnp.dot(to_rows, dir_pair, preferred_element_type=jnp.float32).astype(
                jnp.bfloat16
            )
            for slot_id in range(2):
                spill_out = bf16x3_apply(spill_high[slot_id], spill_mid[slot_id], moved, cols)
                out_high = lax.reduce_precision(spill_out, exponent_bits=8, mantissa_bits=7)
                out_rest = spill_out - out_high
                out_mid = lax.reduce_precision(out_rest, exponent_bits=8, mantissa_bits=7)
                pieces = jnp.concatenate([out_high, out_mid, out_rest - out_mid], axis=1)
                placed = jnp.dot(
                    spill_place[:, slot_id * tile_rows : (slot_id + 1) * tile_rows],
                    pieces.astype(jnp.bfloat16),
                    preferred_element_type=jnp.float32,
                )
                local = local + (
                    (placed[:, :cols] + placed[:, cols : 2 * cols]) + placed[:, 2 * cols :]
                )
        else:
            local = bf16x3_apply(op_high, op_mid, dir_pair, cols)
        faces = [local[face_id * width : (face_id + 1) * width] for face_id in range(4)]
        residual = residual - face_sum_parts(faces)
        if step_id + 1 < ITERS:
            rho_next = 1.0 / (2.0 * sigma_value - rho_value)
            direction = rho_next * rho_value * direction + 2.0 * rho_next / half_width * residual
            rho_value = rho_next
    return (solution[None, None], residual[None, None])


def solution(mesh):
    in_specs = (
        P("gx", "gy", None, None),
        P("gx", "gy", None, None),
        P("gx", "gy", None, None, None),
        P("gx", "gy", None),
        P("gx", "gy"),
        P("gx", "gy", None),
    )
    out_specs = (P("gx", "gy", None, None), P("gx", "gy", None, None))
    return jax.shard_map(body, mesh=mesh, in_specs=in_specs, out_specs=out_specs, check_vma=False)
```

```python
import jax
import jax.numpy as jnp
from jax import lax
from jax.sharding import PartitionSpec as P

ITERS = 4


low_bound = 0.5
high_bound = 7.0


def shifted(block, axis, distance):
    devices = range(lax.axis_size(axis))
    route = [(i - distance, i) for i in devices if i - distance in devices]
    return lax.ppermute(block, axis, route)


def from_behind(value, axis, steps):
    count = lax.axis_size(axis)
    pairs = [(source, (source + steps) % count) for source in range(count)]
    return lax.ppermute(value, axis, pairs)


def along_x(part, offset):
    return shifted(part, "gx", offset)


def along_y(part, offset):
    return shifted(part, "gy", offset)


def face_sum(local):
    width = local.shape[0] // 4
    low_x = local[0:width]
    high_x = local[width : 2 * width]
    low_y = local[2 * width : 3 * width]
    high_y = local[3 * width : 4 * width]
    return jnp.concatenate(
        [
            low_x + along_x(high_x, 1),
            high_x + along_x(low_x, -1),
            low_y + along_y(high_y, 1),
            high_y + along_y(low_y, -1),
        ],
        axis=0,
    )


def swap_pairs(count, first):
    pairs = []
    for low in range(first, count - 1, 2):
        pairs += [(low, low + 1), (low + 1, low)]
    return pairs


def face_sum_parts(faces, one_axis_at_a_time=False):
    low_x, high_x, low_y, high_y = faces
    sides = [(low_y, high_y, "gy"), (low_x, high_x, "gx")]
    sends = []
    for low, high, axis in sides:
        even = lax.axis_index(axis) % 2 == 0
        sends.append((jnp.where(even, low, high), swap_pairs(lax.axis_size(axis), 1), axis))
        sends.append((jnp.where(even, high, low), swap_pairs(lax.axis_size(axis), 0), axis))
    if one_axis_at_a_time:
        rest = [sends[0], sends[1], sends[3]]
        first = lax.ppermute(sends[2][0], sends[2][2], sends[2][1])
        later, first = lax.optimization_barrier(([block for block, _, _ in rest], first))
        second = [
            lax.ppermute(block, axis, pairs) for block, (_, pairs, axis) in zip(later, rest)
        ]
        received = lax.optimization_barrier([second[0], second[1], first, second[2]])
    else:
        received = lax.optimization_barrier(
            [lax.ppermute(block, axis, pairs) for block, pairs, axis in sends]
        )
    summed = []
    for side_id, (low, high, axis) in enumerate(sides):
        even = lax.axis_index(axis) % 2 == 0
        odd_recv, even_recv = received[2 * side_id], received[2 * side_id + 1]
        summed.append(low + jnp.where(even, odd_recv, even_recv))
        summed.append(high + jnp.where(even, even_recv, odd_recv))
    new_low_y, new_high_y, new_low_x, new_high_x = summed
    return jnp.concatenate([new_low_x, new_high_x, new_low_y, new_high_y], axis=0)


def slot_pieces(rows, to_rows, to_slots):
    high = lax.reduce_precision(rows, exponent_bits=8, mantissa_bits=7)
    mid = lax.reduce_precision(rows - high, exponent_bits=8, mantissa_bits=7)
    count = rows.shape[0]
    stacked = jnp.concatenate([high, mid], axis=0).astype(jnp.bfloat16)
    by_cols = jnp.dot(stacked, to_rows, preferred_element_type=jnp.float32).astype(jnp.bfloat16)
    side = jnp.concatenate([by_cols[:count], by_cols[count:]], axis=1)
    return jnp.dot(to_slots, side, preferred_element_type=jnp.float32)


def bf16x3_apply(op_high, op_mid, pair, cols):
    both = jnp.dot(op_high, pair, preferred_element_type=jnp.float32)
    return (both[:, :cols] + both[:, cols:]) + jnp.dot(
        op_mid, pair[:, :cols], preferred_element_type=jnp.float32
    )


def body(gap, own_rows, spill_rows, tile_plan, orders, slot_rows):
    order_max = gap.shape[2]
    tile_rows = spill_rows.shape[3]
    own_tiles = own_rows.shape[2] // tile_rows
    hop_span = lax.axis_size("gx") // 4
    own_block = own_rows[0, 0]
    spill_block = spill_rows[0, 0]
    plan_row = tile_plan[0, 0]
    order_now = orders[0, 0]
    slot_map = slot_rows[0, 0]
    row_ids = jnp.arange(order_max, dtype=jnp.int32)
    face_sign = jnp.where(row_ids // (order_max // 4) % 2 == 0, -1.0, 1.0).astype(jnp.float32)
    slot_scale = face_sign * (slot_map < order_now).astype(jnp.float32)
    spill_parts = [spill_block[slot_id] for slot_id in range(2)]
    gap_faces, spill_parts = lax.optimization_barrier((gap[0, 0], spill_parts))
    homed = [
        from_behind(spill_parts[slot_id], "gx", -(slot_id + 1) * hop_span) for slot_id in range(2)
    ]
    own_count = own_block.shape[0]
    cols = gap.shape[3]
    width = order_max // 4
    load = face_sum_parts(
        [gap_faces[face_id * width : (face_id + 1) * width] for face_id in range(4)],
        one_axis_at_a_time=True,
    )
    to_slots = jnp.where(
        slot_map[:, None] == row_ids[None, :], slot_scale[:, None], 0.0
    ).astype(jnp.bfloat16)
    to_rows = jnp.where(
        row_ids[:, None] == slot_map[None, :], slot_scale[None, :], 0.0
    ).astype(jnp.bfloat16)
    own_slots = slot_pieces(own_block, to_rows, to_slots[:, :own_count])
    spill_ids = jnp.concatenate(
        [
            jnp.where(plan_row[slot_id] >= own_tiles, plan_row[slot_id] * tile_rows, -order_max)
            + jnp.arange(tile_rows, dtype=jnp.int32)
            for slot_id in range(2)
        ]
    )
    spill_place = jnp.where(
        slot_map[:, None] == spill_ids[None, :], slot_scale[:, None], 0.0
    ).astype(jnp.bfloat16)
    spill_slots = [
        slot_pieces(homed[slot_id], to_rows, spill_place[:, slot_id * tile_rows : (slot_id + 1) * tile_rows])
        for slot_id in range(2)
    ]
    own_high = own_slots[:, :order_max].astype(jnp.bfloat16)
    own_mid = own_slots[:, order_max:].astype(jnp.bfloat16)
    full_slots = own_slots + (spill_slots[0] + spill_slots[1])
    op_high = full_slots[:, :order_max].astype(jnp.bfloat16)
    op_mid = full_slots[:, order_max:].astype(jnp.bfloat16)
    spill_high = [lax.reduce_precision(block, exponent_bits=8, mantissa_bits=7) for block in homed]
    spill_mid = [(block - high).astype(jnp.bfloat16) for block, high in zip(homed, spill_high)]
    spill_high = [high.astype(jnp.bfloat16) for high in spill_high]
    centre = (high_bound + low_bound) / 2.0
    half_width = (high_bound - low_bound) / 2.0
    sigma_value = centre / half_width
    rho_value = 1.0 / sigma_value
    solution = jnp.zeros_like(load)
    residual = load
    direction = residual / centre
    for step_id in range(ITERS):
        solution = solution + direction
        dir_high = lax.reduce_precision(direction, exponent_bits=8, mantissa_bits=7)
        dir_pair = jnp.concatenate([dir_high, direction - dir_high], axis=1).astype(jnp.bfloat16)
        if step_id == 0:
            local = bf16x3_apply(own_high, own_mid, dir_pair, cols)
            moved = jnp.dot(to_rows, dir_pair, preferred_element_type=jnp.float32).astype(
                jnp.bfloat16
            )
            for slot_id in range(2):
                spill_out = bf16x3_apply(spill_high[slot_id], spill_mid[slot_id], moved, cols)
                out_high = lax.reduce_precision(spill_out, exponent_bits=8, mantissa_bits=7)
                out_rest = spill_out - out_high
                out_mid = lax.reduce_precision(out_rest, exponent_bits=8, mantissa_bits=7)
                pieces = jnp.concatenate([out_high, out_mid, out_rest - out_mid], axis=1)
                placed = jnp.dot(
                    spill_place[:, slot_id * tile_rows : (slot_id + 1) * tile_rows],
                    pieces.astype(jnp.bfloat16),
                    preferred_element_type=jnp.float32,
                )
                local = local + (
                    (placed[:, :cols] + placed[:, cols : 2 * cols]) + placed[:, 2 * cols :]
                )
        else:
            local = bf16x3_apply(op_high, op_mid, dir_pair, cols)
        faces = [local[face_id * width : (face_id + 1) * width] for face_id in range(4)]
        residual = residual - face_sum_parts(faces)
        if step_id + 1 < ITERS:
            rho_next = 1.0 / (2.0 * sigma_value - rho_value)
            direction = rho_next * rho_value * direction + 2.0 * rho_next / half_width * residual
            rho_value = rho_next
    return (solution[None, None], residual[None, None])


def solution(mesh):
    in_specs = (
        P("gx", "gy", None, None),
        P("gx", "gy", None, None),
        P("gx", "gy", None, None, None),
        P("gx", "gy", None),
        P("gx", "gy"),
        P("gx", "gy", None),
    )
    out_specs = (P("gx", "gy", None, None), P("gx", "gy", None, None))
    return jax.shard_map(body, mesh=mesh, in_specs=in_specs, out_specs=out_specs, check_vma=False)
```

```python
import jax
import jax.numpy as jnp
from jax import lax
from jax.sharding import PartitionSpec as P

ITERS = 4


low_bound = 0.5
high_bound = 7.0


def shifted(block, axis, distance):
    devices = range(lax.axis_size(axis))
    route = [(i - distance, i) for i in devices if i - distance in devices]
    return lax.ppermute(block, axis, route)


def from_behind(value, axis, steps):
    count = lax.axis_size(axis)
    pairs = [(source, (source + steps) % count) for source in range(count)]
    return lax.ppermute(value, axis, pairs)


def along_x(part, offset):
    return shifted(part, "gx", offset)


def along_y(part, offset):
    return shifted(part, "gy", offset)


def face_sum(local):
    width = local.shape[0] // 4
    low_x = local[0:width]
    high_x = local[width : 2 * width]
    low_y = local[2 * width : 3 * width]
    high_y = local[3 * width : 4 * width]
    return jnp.concatenate(
        [
            low_x + along_x(high_x, 1),
            high_x + along_x(low_x, -1),
            low_y + along_y(high_y, 1),
            high_y + along_y(low_y, -1),
        ],
        axis=0,
    )


def swap_pairs(count, first):
    pairs = []
    for low in range(first, count - 1, 2):
        pairs += [(low, low + 1), (low + 1, low)]
    return pairs


def face_sum_parts(faces, one_axis_at_a_time=False):
    low_x, high_x, low_y, high_y = faces
    sides = [(low_y, high_y, "gy"), (low_x, high_x, "gx")]
    sends = []
    for low, high, axis in sides:
        even = lax.axis_index(axis) % 2 == 0
        sends.append((jnp.where(even, low, high), swap_pairs(lax.axis_size(axis), 1), axis))
        sends.append((jnp.where(even, high, low), swap_pairs(lax.axis_size(axis), 0), axis))
    if one_axis_at_a_time:
        first = [lax.ppermute(block, axis, pairs) for block, pairs, axis in sends[2:]]
        later, first = lax.optimization_barrier(([block for block, _, _ in sends[:2]], first))
        second = [
            lax.ppermute(block, axis, pairs)
            for block, (_, pairs, axis) in zip(later, sends[:2])
        ]
        received = lax.optimization_barrier(second + first)
    else:
        received = lax.optimization_barrier(
            [lax.ppermute(block, axis, pairs) for block, pairs, axis in sends]
        )
    summed = []
    for side_id, (low, high, axis) in enumerate(sides):
        even = lax.axis_index(axis) % 2 == 0
        odd_recv, even_recv = received[2 * side_id], received[2 * side_id + 1]
        summed.append(low + jnp.where(even, odd_recv, even_recv))
        summed.append(high + jnp.where(even, even_recv, odd_recv))
    new_low_y, new_high_y, new_low_x, new_high_x = summed
    return jnp.concatenate([new_low_x, new_high_x, new_low_y, new_high_y], axis=0)


def slot_pieces(rows, to_rows, to_slots):
    high = lax.reduce_precision(rows, exponent_bits=8, mantissa_bits=7)
    mid = lax.reduce_precision(rows - high, exponent_bits=8, mantissa_bits=7)
    count = rows.shape[0]
    stacked = jnp.concatenate([high, mid], axis=0).astype(jnp.bfloat16)
    by_cols = jnp.dot(stacked, to_rows, preferred_element_type=jnp.float32).astype(jnp.bfloat16)
    side = jnp.concatenate([by_cols[:count], by_cols[count:]], axis=1)
    return jnp.dot(to_slots, side, preferred_element_type=jnp.float32)


def bf16x3_apply(op_high, op_mid, pair, cols):
    both = jnp.dot(op_high, pair, preferred_element_type=jnp.float32)
    return (both[:, :cols] + both[:, cols:]) + jnp.dot(
        op_mid, pair[:, :cols], preferred_element_type=jnp.float32
    )


def body(gap, own_rows, spill_rows, tile_plan, orders, slot_rows):
    order_max = gap.shape[2]
    tile_rows = spill_rows.shape[3]
    own_tiles = own_rows.shape[2] // tile_rows
    hop_span = lax.axis_size("gx") // 4
    own_block = own_rows[0, 0]
    spill_block = spill_rows[0, 0]
    plan_row = tile_plan[0, 0]
    order_now = orders[0, 0]
    slot_map = slot_rows[0, 0]
    row_ids = jnp.arange(order_max, dtype=jnp.int32)
    face_sign = jnp.where(row_ids // (order_max // 4) % 2 == 0, -1.0, 1.0).astype(jnp.float32)
    slot_scale = face_sign * (slot_map < order_now).astype(jnp.float32)
    spill_parts = [spill_block[slot_id] for slot_id in range(2)]
    gap_faces, spill_parts = lax.optimization_barrier((gap[0, 0], spill_parts))
    homed = [
        from_behind(spill_parts[slot_id], "gx", -(slot_id + 1) * hop_span) for slot_id in range(2)
    ]
    own_count = own_block.shape[0]
    cols = gap.shape[3]
    width = order_max // 4
    load = face_sum_parts(
        [gap_faces[face_id * width : (face_id + 1) * width] for face_id in range(4)],
        one_axis_at_a_time=True,
    )
    to_slots = jnp.where(
        slot_map[:, None] == row_ids[None, :], slot_scale[:, None], 0.0
    ).astype(jnp.bfloat16)
    to_rows = jnp.where(
        row_ids[:, None] == slot_map[None, :], slot_scale[None, :], 0.0
    ).astype(jnp.bfloat16)
    own_slots = slot_pieces(own_block, to_rows, to_slots[:, :own_count])
    spill_ids = jnp.concatenate(
        [
            jnp.where(plan_row[slot_id] >= own_tiles, plan_row[slot_id] * tile_rows, -order_max)
            + jnp.arange(tile_rows, dtype=jnp.int32)
            for slot_id in range(2)
        ]
    )
    spill_place = jnp.where(
        slot_map[:, None] == spill_ids[None, :], slot_scale[:, None], 0.0
    ).astype(jnp.bfloat16)
    spill_slots = [
        slot_pieces(homed[slot_id], to_rows, spill_place[:, slot_id * tile_rows : (slot_id + 1) * tile_rows])
        for slot_id in range(2)
    ]
    own_high = own_slots[:, :order_max].astype(jnp.bfloat16)
    own_mid = own_slots[:, order_max:].astype(jnp.bfloat16)
    full_slots = own_slots + (spill_slots[0] + spill_slots[1])
    op_high = full_slots[:, :order_max].astype(jnp.bfloat16)
    op_mid = full_slots[:, order_max:].astype(jnp.bfloat16)
    spill_high = [lax.reduce_precision(block, exponent_bits=8, mantissa_bits=7) for block in homed]
    spill_mid = [(block - high).astype(jnp.bfloat16) for block, high in zip(homed, spill_high)]
    spill_high = [high.astype(jnp.bfloat16) for high in spill_high]
    centre = (high_bound + low_bound) / 2.0
    half_width = (high_bound - low_bound) / 2.0
    sigma_value = centre / half_width
    rho_value = 1.0 / sigma_value
    solution = jnp.zeros_like(load)
    residual = load
    direction = residual / centre
    for step_id in range(ITERS):
        solution = solution + direction
        dir_high = lax.reduce_precision(direction, exponent_bits=8, mantissa_bits=7)
        dir_pair = jnp.concatenate([dir_high, direction - dir_high], axis=1).astype(jnp.bfloat16)
        if step_id == 0:
            local = bf16x3_apply(own_high, own_mid, dir_pair, cols)
            moved = jnp.dot(to_rows, dir_pair, preferred_element_type=jnp.float32).astype(
                jnp.bfloat16
            )
            for slot_id in range(2):
                spill_out = bf16x3_apply(spill_high[slot_id], spill_mid[slot_id], moved, cols)
                out_high = lax.reduce_precision(spill_out, exponent_bits=8, mantissa_bits=7)
                out_rest = spill_out - out_high
                out_mid = lax.reduce_precision(out_rest, exponent_bits=8, mantissa_bits=7)
                pieces = jnp.concatenate([out_high, out_mid, out_rest - out_mid], axis=1)
                placed = jnp.dot(
                    spill_place[:, slot_id * tile_rows : (slot_id + 1) * tile_rows],
                    pieces.astype(jnp.bfloat16),
                    preferred_element_type=jnp.float32,
                )
                local = local + (
                    (placed[:, :cols] + placed[:, cols : 2 * cols]) + placed[:, 2 * cols :]
                )
        else:
            local = None
        if local is None:
            y_faces = bf16x3_apply(op_high[2 * width :], op_mid[2 * width :], dir_pair, cols)
            x_faces = bf16x3_apply(op_high[: 2 * width], op_mid[: 2 * width], dir_pair, cols)
            faces = [x_faces[:width], x_faces[width:], y_faces[:width], y_faces[width:]]
        else:
            faces = [local[face_id * width : (face_id + 1) * width] for face_id in range(4)]
        residual = residual - face_sum_parts(faces)
        if step_id + 1 < ITERS:
            rho_next = 1.0 / (2.0 * sigma_value - rho_value)
            direction = rho_next * rho_value * direction + 2.0 * rho_next / half_width * residual
            rho_value = rho_next
    return (solution[None, None], residual[None, None])


def solution(mesh):
    in_specs = (
        P("gx", "gy", None, None),
        P("gx", "gy", None, None),
        P("gx", "gy", None, None, None),
        P("gx", "gy", None),
        P("gx", "gy"),
        P("gx", "gy", None),
    )
    out_specs = (P("gx", "gy", None, None), P("gx", "gy", None, None))
    return jax.shard_map(body, mesh=mesh, in_specs=in_specs, out_specs=out_specs, check_vma=False)
```

```python
import jax
import jax.numpy as jnp
from jax import lax
from jax.sharding import PartitionSpec as P

ITERS = 4


low_bound = 0.5
high_bound = 7.0


def shifted(block, axis, distance):
    devices = range(lax.axis_size(axis))
    route = [(i - distance, i) for i in devices if i - distance in devices]
    return lax.ppermute(block, axis, route)


def from_behind(value, axis, steps):
    count = lax.axis_size(axis)
    pairs = [(source, (source + steps) % count) for source in range(count)]
    return lax.ppermute(value, axis, pairs)


def along_x(part, offset):
    return shifted(part, "gx", offset)


def along_y(part, offset):
    return shifted(part, "gy", offset)


def face_sum(local):
    width = local.shape[0] // 4
    low_x = local[0:width]
    high_x = local[width : 2 * width]
    low_y = local[2 * width : 3 * width]
    high_y = local[3 * width : 4 * width]
    return jnp.concatenate(
        [
            low_x + along_x(high_x, 1),
            high_x + along_x(low_x, -1),
            low_y + along_y(high_y, 1),
            high_y + along_y(low_y, -1),
        ],
        axis=0,
    )


def swap_pairs(count, first):
    pairs = []
    for low in range(first, count - 1, 2):
        pairs += [(low, low + 1), (low + 1, low)]
    return pairs


def face_sum_parts(faces, one_axis_at_a_time=False):
    low_x, high_x, low_y, high_y = faces
    sides = [(low_y, high_y, "gy"), (low_x, high_x, "gx")]
    sends = []
    for low, high, axis in sides:
        even = lax.axis_index(axis) % 2 == 0
        sends.append((jnp.where(even, low, high), swap_pairs(lax.axis_size(axis), 1), axis))
        sends.append((jnp.where(even, high, low), swap_pairs(lax.axis_size(axis), 0), axis))
    if one_axis_at_a_time:
        first = [lax.ppermute(block, axis, pairs) for block, pairs, axis in sends[2:]]
        later, first = lax.optimization_barrier(([block for block, _, _ in sends[:2]], first))
        second = [
            lax.ppermute(block, axis, pairs)
            for block, (_, pairs, axis) in zip(later, sends[:2])
        ]
        received = lax.optimization_barrier(second + first)
    else:
        received = lax.optimization_barrier(
            [lax.ppermute(block, axis, pairs) for block, pairs, axis in sends]
        )
    summed = []
    for side_id, (low, high, axis) in enumerate(sides):
        even = lax.axis_index(axis) % 2 == 0
        odd_recv, even_recv = received[2 * side_id], received[2 * side_id + 1]
        summed.append(low + jnp.where(even, odd_recv, even_recv))
        summed.append(high + jnp.where(even, even_recv, odd_recv))
    new_low_y, new_high_y, new_low_x, new_high_x = summed
    return jnp.concatenate([new_low_x, new_high_x, new_low_y, new_high_y], axis=0)


def slot_pieces(rows, to_rows, to_slots):
    high = lax.reduce_precision(rows, exponent_bits=8, mantissa_bits=7)
    mid = lax.reduce_precision(rows - high, exponent_bits=8, mantissa_bits=7)
    count = rows.shape[0]
    stacked = jnp.concatenate([high, mid], axis=0).astype(jnp.bfloat16)
    by_cols = jnp.dot(stacked, to_rows, preferred_element_type=jnp.float32).astype(jnp.bfloat16)
    side = jnp.concatenate([by_cols[:count], by_cols[count:]], axis=1)
    return jnp.dot(to_slots, side, preferred_element_type=jnp.float32)


def bf16x3_apply(op_high, op_mid, pair, cols):
    both = jnp.dot(op_high, pair, preferred_element_type=jnp.float32)
    return (both[:, :cols] + both[:, cols:]) + jnp.dot(
        op_mid, pair[:, :cols], preferred_element_type=jnp.float32
    )


def body(gap, own_rows, spill_rows, tile_plan, orders, slot_rows):
    order_max = gap.shape[2]
    tile_rows = spill_rows.shape[3]
    own_tiles = own_rows.shape[2] // tile_rows
    hop_span = lax.axis_size("gx") // 4
    own_block = own_rows[0, 0]
    spill_block = spill_rows[0, 0]
    plan_row = tile_plan[0, 0]
    order_now = orders[0, 0]
    slot_map = slot_rows[0, 0]
    row_ids = jnp.arange(order_max, dtype=jnp.int32)
    face_sign = jnp.where(row_ids // (order_max // 4) % 2 == 0, -1.0, 1.0).astype(jnp.float32)
    slot_scale = face_sign * (slot_map < order_now).astype(jnp.float32)
    spill_parts = [spill_block[slot_id] for slot_id in range(2)]
    gap_faces, spill_parts = lax.optimization_barrier((gap[0, 0], spill_parts))
    homed = [
        from_behind(spill_parts[slot_id], "gx", -(slot_id + 1) * hop_span) for slot_id in range(2)
    ]
    own_count = own_block.shape[0]
    cols = gap.shape[3]
    width = order_max // 4
    load = face_sum_parts(
        [gap_faces[face_id * width : (face_id + 1) * width] for face_id in range(4)],
        one_axis_at_a_time=True,
    )
    to_slots = jnp.where(
        slot_map[:, None] == row_ids[None, :], slot_scale[:, None], 0.0
    ).astype(jnp.bfloat16)
    to_rows = jnp.where(
        row_ids[:, None] == slot_map[None, :], slot_scale[None, :], 0.0
    ).astype(jnp.bfloat16)
    own_slots = slot_pieces(own_block, to_rows, to_slots[:, :own_count])
    spill_ids = jnp.concatenate(
        [
            jnp.where(plan_row[slot_id] >= own_tiles, plan_row[slot_id] * tile_rows, -order_max)
            + jnp.arange(tile_rows, dtype=jnp.int32)
            for slot_id in range(2)
        ]
    )
    spill_place = jnp.where(
        slot_map[:, None] == spill_ids[None, :], slot_scale[:, None], 0.0
    ).astype(jnp.bfloat16)
    spill_stack = jnp.concatenate(homed, axis=0)
    spill_slots = slot_pieces(spill_stack, to_rows, spill_place)
    own_cat = jnp.concatenate(
        [own_slots[:, :order_max], own_slots[:, :order_max], own_slots[:, order_max:]], axis=1
    ).astype(jnp.bfloat16)
    full_slots = own_slots + spill_slots
    op_cat = jnp.concatenate(
        [full_slots[:, :order_max], full_slots[:, :order_max], full_slots[:, order_max:]], axis=1
    ).astype(jnp.bfloat16)
    spill_high = lax.reduce_precision(spill_stack, exponent_bits=8, mantissa_bits=7)
    spill_mid = (spill_stack - spill_high).astype(jnp.bfloat16)
    spill_high = spill_high.astype(jnp.bfloat16)
    centre = (high_bound + low_bound) / 2.0
    half_width = (high_bound - low_bound) / 2.0
    sigma_value = centre / half_width
    rho_value = 1.0 / sigma_value
    solution = jnp.zeros_like(load)
    residual = load
    direction = residual / centre
    for step_id in range(ITERS):
        solution = solution + direction
        dir_high = lax.reduce_precision(direction, exponent_bits=8, mantissa_bits=7)
        dir_pair = jnp.concatenate([dir_high, direction - dir_high], axis=1).astype(jnp.bfloat16)
        dir_stack = jnp.concatenate(
            [dir_high, direction - dir_high, dir_high], axis=0
        ).astype(jnp.bfloat16)
        if step_id == 0:
            local = jnp.dot(own_cat, dir_stack, preferred_element_type=jnp.float32)
            moved = jnp.dot(to_rows, dir_pair, preferred_element_type=jnp.float32).astype(
                jnp.bfloat16
            )
            spill_out = bf16x3_apply(spill_high, spill_mid, moved, cols)
            out_high = lax.reduce_precision(spill_out, exponent_bits=8, mantissa_bits=7)
            out_rest = spill_out - out_high
            out_mid = lax.reduce_precision(out_rest, exponent_bits=8, mantissa_bits=7)
            pieces = jnp.concatenate([out_high, out_mid, out_rest - out_mid], axis=1)
            placed = jnp.dot(
                spill_place, pieces.astype(jnp.bfloat16), preferred_element_type=jnp.float32
            )
            local = local + (
                (placed[:, :cols] + placed[:, cols : 2 * cols]) + placed[:, 2 * cols :]
            )
        else:
            local = jnp.dot(op_cat, dir_stack, preferred_element_type=jnp.float32)
        faces = [local[face_id * width : (face_id + 1) * width] for face_id in range(4)]
        residual = residual - face_sum_parts(faces)
        if step_id + 1 < ITERS:
            rho_next = 1.0 / (2.0 * sigma_value - rho_value)
            direction = rho_next * rho_value * direction + 2.0 * rho_next / half_width * residual
            rho_value = rho_next
    return (solution[None, None], residual[None, None])


def solution(mesh):
    in_specs = (
        P("gx", "gy", None, None),
        P("gx", "gy", None, None),
        P("gx", "gy", None, None, None),
        P("gx", "gy", None),
        P("gx", "gy"),
        P("gx", "gy", None),
    )
    out_specs = (P("gx", "gy", None, None), P("gx", "gy", None, None))
    return jax.shard_map(body, mesh=mesh, in_specs=in_specs, out_specs=out_specs, check_vma=False)
```

```python
import jax
import jax.numpy as jnp
from jax import lax
from jax.sharding import PartitionSpec as P

ITERS = 4


low_bound = 0.5
high_bound = 7.0


def shifted(block, axis, distance):
    devices = range(lax.axis_size(axis))
    route = [(i - distance, i) for i in devices if i - distance in devices]
    return lax.ppermute(block, axis, route)


def from_behind(value, axis, steps):
    count = lax.axis_size(axis)
    pairs = [(source, (source + steps) % count) for source in range(count)]
    return lax.ppermute(value, axis, pairs)


def along_x(part, offset):
    return shifted(part, "gx", offset)


def along_y(part, offset):
    return shifted(part, "gy", offset)


def face_sum(local):
    width = local.shape[0] // 4
    low_x = local[0:width]
    high_x = local[width : 2 * width]
    low_y = local[2 * width : 3 * width]
    high_y = local[3 * width : 4 * width]
    return jnp.concatenate(
        [
            low_x + along_x(high_x, 1),
            high_x + along_x(low_x, -1),
            low_y + along_y(high_y, 1),
            high_y + along_y(low_y, -1),
        ],
        axis=0,
    )


def swap_pairs(count, first):
    pairs = []
    for low in range(first, count - 1, 2):
        pairs += [(low, low + 1), (low + 1, low)]
    return pairs


def face_sum_parts(faces, one_axis_at_a_time=False):
    low_x, high_x, low_y, high_y = faces
    sides = [(low_y, high_y, "gy"), (low_x, high_x, "gx")]
    sends = []
    for low, high, axis in sides:
        even = lax.axis_index(axis) % 2 == 0
        sends.append((jnp.where(even, low, high), swap_pairs(lax.axis_size(axis), 1), axis))
        sends.append((jnp.where(even, high, low), swap_pairs(lax.axis_size(axis), 0), axis))
    if one_axis_at_a_time:
        first = [lax.ppermute(block, axis, pairs) for block, pairs, axis in sends[2:]]
        later, first = lax.optimization_barrier(([block for block, _, _ in sends[:2]], first))
        second = [
            lax.ppermute(block, axis, pairs)
            for block, (_, pairs, axis) in zip(later, sends[:2])
        ]
        received = lax.optimization_barrier(second + first)
    else:
        received = lax.optimization_barrier(
            [lax.ppermute(block, axis, pairs) for block, pairs, axis in sends]
        )
    summed = []
    for side_id, (low, high, axis) in enumerate(sides):
        even = lax.axis_index(axis) % 2 == 0
        odd_recv, even_recv = received[2 * side_id], received[2 * side_id + 1]
        summed.append(low + jnp.where(even, odd_recv, even_recv))
        summed.append(high + jnp.where(even, even_recv, odd_recv))
    new_low_y, new_high_y, new_low_x, new_high_x = summed
    return jnp.concatenate([new_low_x, new_high_x, new_low_y, new_high_y], axis=0)


def slot_pieces(rows, to_rows, to_slots):
    high = lax.reduce_precision(rows, exponent_bits=8, mantissa_bits=7)
    mid = lax.reduce_precision(rows - high, exponent_bits=8, mantissa_bits=7)
    count = rows.shape[0]
    stacked = jnp.concatenate([high, mid], axis=0).astype(jnp.bfloat16)
    by_cols = jnp.dot(stacked, to_rows, preferred_element_type=jnp.float32).astype(jnp.bfloat16)
    side = jnp.concatenate([by_cols[:count], by_cols[count:]], axis=1)
    return jnp.dot(to_slots, side, preferred_element_type=jnp.float32)


def bf16x3_apply(op_high, op_mid, pair, cols):
    both = jnp.dot(op_high, pair, preferred_element_type=jnp.float32)
    return (both[:, :cols] + both[:, cols:]) + jnp.dot(
        op_mid, pair[:, :cols], preferred_element_type=jnp.float32
    )


def body(gap, own_rows, spill_rows, tile_plan, orders, slot_rows):
    order_max = gap.shape[2]
    tile_rows = spill_rows.shape[3]
    own_tiles = own_rows.shape[2] // tile_rows
    hop_span = lax.axis_size("gx") // 4
    own_block = own_rows[0, 0]
    spill_block = spill_rows[0, 0]
    plan_row = tile_plan[0, 0]
    order_now = orders[0, 0]
    slot_map = slot_rows[0, 0]
    row_ids = jnp.arange(order_max, dtype=jnp.int32)
    face_sign = jnp.where(row_ids // (order_max // 4) % 2 == 0, -1.0, 1.0).astype(jnp.float32)
    slot_scale = face_sign * (slot_map < order_now).astype(jnp.float32)
    spill_parts = [spill_block[slot_id] for slot_id in range(2)]
    gap_faces = gap[0, 0]
    homed = [
        from_behind(spill_parts[slot_id], "gx", -(slot_id + 1) * hop_span) for slot_id in range(2)
    ]
    own_count = own_block.shape[0]
    cols = gap.shape[3]
    width = order_max // 4
    load = face_sum_parts(
        [gap_faces[face_id * width : (face_id + 1) * width] for face_id in range(4)],
        one_axis_at_a_time=True,
    )
    to_slots = jnp.where(
        slot_map[:, None] == row_ids[None, :], slot_scale[:, None], 0.0
    ).astype(jnp.bfloat16)
    to_rows = jnp.where(
        row_ids[:, None] == slot_map[None, :], slot_scale[None, :], 0.0
    ).astype(jnp.bfloat16)
    own_slots = slot_pieces(own_block, to_rows, to_slots[:, :own_count])
    spill_ids = jnp.concatenate(
        [
            jnp.where(plan_row[slot_id] >= own_tiles, plan_row[slot_id] * tile_rows, -order_max)
            + jnp.arange(tile_rows, dtype=jnp.int32)
            for slot_id in range(2)
        ]
    )
    spill_place = jnp.where(
        slot_map[:, None] == spill_ids[None, :], slot_scale[:, None], 0.0
    ).astype(jnp.bfloat16)
    spill_stack = jnp.concatenate(homed, axis=0)
    spill_slots = slot_pieces(spill_stack, to_rows, spill_place)
    own_high = own_slots[:, :order_max].astype(jnp.bfloat16)
    own_mid = own_slots[:, order_max:].astype(jnp.bfloat16)
    op_high = (own_slots[:, :order_max] + spill_slots[:, :order_max]).astype(jnp.bfloat16)
    op_mid = (own_slots[:, order_max:] + spill_slots[:, order_max:]).astype(jnp.bfloat16)
    spill_high = lax.reduce_precision(spill_stack, exponent_bits=8, mantissa_bits=7)
    spill_mid = (spill_stack - spill_high).astype(jnp.bfloat16)
    spill_high = spill_high.astype(jnp.bfloat16)
    centre = (high_bound + low_bound) / 2.0
    half_width = (high_bound - low_bound) / 2.0
    sigma_value = centre / half_width
    rho_value = 1.0 / sigma_value
    solution = jnp.zeros_like(load)
    residual = load
    direction = residual / centre
    for step_id in range(ITERS):
        solution = solution + direction
        dir_high = lax.reduce_precision(direction, exponent_bits=8, mantissa_bits=7)
        dir_pair = jnp.concatenate([dir_high, direction - dir_high], axis=1).astype(jnp.bfloat16)
        if step_id == 0:
            local = bf16x3_apply(own_high, own_mid, dir_pair, cols)
            moved = jnp.dot(to_rows, dir_pair, preferred_element_type=jnp.float32).astype(
                jnp.bfloat16
            )
            spill_out = bf16x3_apply(spill_high, spill_mid, moved, cols)
            out_high = lax.reduce_precision(spill_out, exponent_bits=8, mantissa_bits=7)
            out_rest = spill_out - out_high
            out_mid = lax.reduce_precision(out_rest, exponent_bits=8, mantissa_bits=7)
            pieces = jnp.concatenate([out_high, out_mid, out_rest - out_mid], axis=1)
            placed = jnp.dot(
                spill_place, pieces.astype(jnp.bfloat16), preferred_element_type=jnp.float32
            )
            local = local + (
                (placed[:, :cols] + placed[:, cols : 2 * cols]) + placed[:, 2 * cols :]
            )
        else:
            local = bf16x3_apply(op_high, op_mid, dir_pair, cols)
        faces = [local[face_id * width : (face_id + 1) * width] for face_id in range(4)]
        residual = residual - face_sum_parts(faces)
        if step_id + 1 < ITERS:
            rho_next = 1.0 / (2.0 * sigma_value - rho_value)
            direction = rho_next * rho_value * direction + 2.0 * rho_next / half_width * residual
            rho_value = rho_next
    return (solution[None, None], residual[None, None])


def solution(mesh):
    in_specs = (
        P("gx", "gy", None, None),
        P("gx", "gy", None, None),
        P("gx", "gy", None, None, None),
        P("gx", "gy", None),
        P("gx", "gy"),
        P("gx", "gy", None),
    )
    out_specs = (P("gx", "gy", None, None), P("gx", "gy", None, None))
    return jax.shard_map(body, mesh=mesh, in_specs=in_specs, out_specs=out_specs, check_vma=False)
```

```python
import jax
import jax.numpy as jnp
from jax import lax
from jax.sharding import PartitionSpec as P

ITERS = 4


low_bound = 0.5
high_bound = 7.0


def shifted(block, axis, distance):
    devices = range(lax.axis_size(axis))
    route = [(i - distance, i) for i in devices if i - distance in devices]
    return lax.ppermute(block, axis, route)


def from_behind(value, axis, steps):
    count = lax.axis_size(axis)
    pairs = [(source, (source + steps) % count) for source in range(count)]
    return lax.ppermute(value, axis, pairs)


def along_x(part, offset):
    return shifted(part, "gx", offset)


def along_y(part, offset):
    return shifted(part, "gy", offset)


def face_sum(local):
    width = local.shape[0] // 4
    low_x = local[0:width]
    high_x = local[width : 2 * width]
    low_y = local[2 * width : 3 * width]
    high_y = local[3 * width : 4 * width]
    return jnp.concatenate(
        [
            low_x + along_x(high_x, 1),
            high_x + along_x(low_x, -1),
            low_y + along_y(high_y, 1),
            high_y + along_y(low_y, -1),
        ],
        axis=0,
    )


def swap_pairs(count, first):
    pairs = []
    for low in range(first, count - 1, 2):
        pairs += [(low, low + 1), (low + 1, low)]
    return pairs


def face_arrivals(faces, one_axis_at_a_time=False):
    low_x, high_x, low_y, high_y = faces
    sides = [(low_y, high_y, "gy"), (low_x, high_x, "gx")]
    sends = []
    for low, high, axis in sides:
        even = lax.axis_index(axis) % 2 == 0
        sends.append((jnp.where(even, low, high), swap_pairs(lax.axis_size(axis), 1), axis))
        sends.append((jnp.where(even, high, low), swap_pairs(lax.axis_size(axis), 0), axis))
    if one_axis_at_a_time:
        first = [lax.ppermute(block, axis, pairs) for block, pairs, axis in sends[2:]]
        later, first = lax.optimization_barrier(([block for block, _, _ in sends[:2]], first))
        second = [
            lax.ppermute(block, axis, pairs)
            for block, (_, pairs, axis) in zip(later, sends[:2])
        ]
        received = lax.optimization_barrier(second + first)
    else:
        received = lax.optimization_barrier(
            [lax.ppermute(block, axis, pairs) for block, pairs, axis in sends]
        )
    arrived = []
    for side_id, (low, high, axis) in enumerate(sides):
        even = lax.axis_index(axis) % 2 == 0
        odd_recv, even_recv = received[2 * side_id], received[2 * side_id + 1]
        arrived.append(jnp.where(even, odd_recv, even_recv))
        arrived.append(jnp.where(even, even_recv, odd_recv))
    from_low_y, from_high_y, from_low_x, from_high_x = arrived
    return jnp.concatenate([from_low_x, from_high_x, from_low_y, from_high_y], axis=0)


def slot_pieces(rows, to_rows, to_slots):
    high = lax.reduce_precision(rows, exponent_bits=8, mantissa_bits=7)
    mid = lax.reduce_precision(rows - high, exponent_bits=8, mantissa_bits=7)
    count = rows.shape[0]
    stacked = jnp.concatenate([high, mid], axis=0).astype(jnp.bfloat16)
    by_cols = jnp.dot(stacked, to_rows, preferred_element_type=jnp.float32).astype(jnp.bfloat16)
    side = jnp.concatenate([by_cols[:count], by_cols[count:]], axis=1)
    return jnp.dot(to_slots, side, preferred_element_type=jnp.float32)


def bf16x3_apply(op_high, op_mid, pair, cols):
    both = jnp.dot(op_high, pair, preferred_element_type=jnp.float32)
    return (both[:, :cols] + both[:, cols:]) + jnp.dot(
        op_mid, pair[:, :cols], preferred_element_type=jnp.float32
    )


def body(gap, own_rows, spill_rows, tile_plan, orders, slot_rows):
    order_max = gap.shape[2]
    tile_rows = spill_rows.shape[3]
    own_tiles = own_rows.shape[2] // tile_rows
    hop_span = lax.axis_size("gx") // 4
    own_block = own_rows[0, 0]
    spill_block = spill_rows[0, 0]
    plan_row = tile_plan[0, 0]
    order_now = orders[0, 0]
    slot_map = slot_rows[0, 0]
    row_ids = jnp.arange(order_max, dtype=jnp.int32)
    face_sign = jnp.where(row_ids // (order_max // 4) % 2 == 0, -1.0, 1.0).astype(jnp.float32)
    slot_scale = face_sign * (slot_map < order_now).astype(jnp.float32)
    spill_parts = [spill_block[slot_id] for slot_id in range(2)]
    gap_faces, spill_parts = lax.optimization_barrier((gap[0, 0], spill_parts))
    homed = [
        from_behind(spill_parts[slot_id], "gx", -(slot_id + 1) * hop_span) for slot_id in range(2)
    ]
    own_count = own_block.shape[0]
    cols = gap.shape[3]
    width = order_max // 4
    load = gap_faces + face_arrivals(
        [gap_faces[face_id * width : (face_id + 1) * width] for face_id in range(4)],
        one_axis_at_a_time=True,
    )
    to_slots = jnp.where(
        slot_map[:, None] == row_ids[None, :], slot_scale[:, None], 0.0
    ).astype(jnp.bfloat16)
    to_rows = jnp.where(
        row_ids[:, None] == slot_map[None, :], slot_scale[None, :], 0.0
    ).astype(jnp.bfloat16)
    own_slots = slot_pieces(own_block, to_rows, to_slots[:, :own_count])
    spill_ids = jnp.concatenate(
        [
            jnp.where(plan_row[slot_id] >= own_tiles, plan_row[slot_id] * tile_rows, -order_max)
            + jnp.arange(tile_rows, dtype=jnp.int32)
            for slot_id in range(2)
        ]
    )
    spill_place = jnp.where(
        slot_map[:, None] == spill_ids[None, :], slot_scale[:, None], 0.0
    ).astype(jnp.bfloat16)
    spill_stack = jnp.concatenate(homed, axis=0)
    spill_slots = slot_pieces(spill_stack, to_rows, spill_place)
    own_high = own_slots[:, :order_max].astype(jnp.bfloat16)
    own_mid = own_slots[:, order_max:].astype(jnp.bfloat16)
    op_high = (own_slots[:, :order_max] + spill_slots[:, :order_max]).astype(jnp.bfloat16)
    op_mid = (own_slots[:, order_max:] + spill_slots[:, order_max:]).astype(jnp.bfloat16)
    spill_high = lax.reduce_precision(spill_stack, exponent_bits=8, mantissa_bits=7)
    spill_mid = (spill_stack - spill_high).astype(jnp.bfloat16)
    spill_high = spill_high.astype(jnp.bfloat16)
    centre = (high_bound + low_bound) / 2.0
    half_width = (high_bound - low_bound) / 2.0
    sigma_value = centre / half_width
    rho_value = 1.0 / sigma_value
    solution = jnp.zeros_like(load)
    residual = load
    direction = residual / centre
    for step_id in range(ITERS):
        solution = solution + direction
        dir_high = lax.reduce_precision(direction, exponent_bits=8, mantissa_bits=7)
        dir_pair = jnp.concatenate([dir_high, direction - dir_high], axis=1).astype(jnp.bfloat16)
        if step_id == 0:
            local = bf16x3_apply(own_high, own_mid, dir_pair, cols)
            moved = jnp.dot(to_rows, dir_pair, preferred_element_type=jnp.float32).astype(
                jnp.bfloat16
            )
            spill_out = bf16x3_apply(spill_high, spill_mid, moved, cols)
            out_high = lax.reduce_precision(spill_out, exponent_bits=8, mantissa_bits=7)
            out_rest = spill_out - out_high
            out_mid = lax.reduce_precision(out_rest, exponent_bits=8, mantissa_bits=7)
            pieces = jnp.concatenate([out_high, out_mid, out_rest - out_mid], axis=1)
            placed = jnp.dot(
                spill_place, pieces.astype(jnp.bfloat16), preferred_element_type=jnp.float32
            )
            local = local + (
                (placed[:, :cols] + placed[:, cols : 2 * cols]) + placed[:, 2 * cols :]
            )
        else:
            local = bf16x3_apply(op_high, op_mid, dir_pair, cols)
        faces = [local[face_id * width : (face_id + 1) * width] for face_id in range(4)]
        residual = (residual - local) - face_arrivals(faces)
        if step_id + 1 < ITERS:
            rho_next = 1.0 / (2.0 * sigma_value - rho_value)
            direction = rho_next * rho_value * direction + 2.0 * rho_next / half_width * residual
            rho_value = rho_next
    return (solution[None, None], residual[None, None])


def solution(mesh):
    in_specs = (
        P("gx", "gy", None, None),
        P("gx", "gy", None, None),
        P("gx", "gy", None, None, None),
        P("gx", "gy", None),
        P("gx", "gy"),
        P("gx", "gy", None),
    )
    out_specs = (P("gx", "gy", None, None), P("gx", "gy", None, None))
    return jax.shard_map(body, mesh=mesh, in_specs=in_specs, out_specs=out_specs, check_vma=False)
```

```python
import jax
import jax.numpy as jnp
from jax import lax
from jax.sharding import PartitionSpec as P

ITERS = 4


low_bound = 0.5
high_bound = 7.0


def shifted(block, axis, distance):
    devices = range(lax.axis_size(axis))
    route = [(i - distance, i) for i in devices if i - distance in devices]
    return lax.ppermute(block, axis, route)


def from_behind(value, axis, steps):
    count = lax.axis_size(axis)
    pairs = [(source, (source + steps) % count) for source in range(count)]
    return lax.ppermute(value, axis, pairs)


def along_x(part, offset):
    return shifted(part, "gx", offset)


def along_y(part, offset):
    return shifted(part, "gy", offset)


def face_sum(local):
    width = local.shape[0] // 4
    low_x = local[0:width]
    high_x = local[width : 2 * width]
    low_y = local[2 * width : 3 * width]
    high_y = local[3 * width : 4 * width]
    return jnp.concatenate(
        [
            low_x + along_x(high_x, 1),
            high_x + along_x(low_x, -1),
            low_y + along_y(high_y, 1),
            high_y + along_y(low_y, -1),
        ],
        axis=0,
    )


def swap_pairs(count, first):
    pairs = []
    for low in range(first, count - 1, 2):
        pairs += [(low, low + 1), (low + 1, low)]
    return pairs


def face_sum_parts(faces, one_axis_at_a_time=False):
    low_x, high_x, low_y, high_y = faces
    sides = [(low_y, high_y, "gy"), (low_x, high_x, "gx")]
    sends = []
    for low, high, axis in sides:
        even = lax.axis_index(axis) % 2 == 0
        sends.append((jnp.where(even, low, high), swap_pairs(lax.axis_size(axis), 1), axis))
        sends.append((jnp.where(even, high, low), swap_pairs(lax.axis_size(axis), 0), axis))
    if one_axis_at_a_time:
        first = [lax.ppermute(block, axis, pairs) for block, pairs, axis in sends[2:]]
        later, first = lax.optimization_barrier(([block for block, _, _ in sends[:2]], first))
        second = [
            lax.ppermute(block, axis, pairs)
            for block, (_, pairs, axis) in zip(later, sends[:2])
        ]
        received = lax.optimization_barrier(second + first)
    else:
        received = lax.optimization_barrier(
            [lax.ppermute(block, axis, pairs) for block, pairs, axis in sends]
        )
    summed = []
    for side_id, (low, high, axis) in enumerate(sides):
        even = lax.axis_index(axis) % 2 == 0
        odd_recv, even_recv = received[2 * side_id], received[2 * side_id + 1]
        summed.append(low + jnp.where(even, odd_recv, even_recv))
        summed.append(high + jnp.where(even, even_recv, odd_recv))
    new_low_y, new_high_y, new_low_x, new_high_x = summed
    return jnp.concatenate([new_low_x, new_high_x, new_low_y, new_high_y], axis=0)


def slot_pieces(rows, to_rows, to_slots):
    high = lax.reduce_precision(rows, exponent_bits=8, mantissa_bits=7)
    mid = lax.reduce_precision(rows - high, exponent_bits=8, mantissa_bits=7)
    count = rows.shape[0]
    stacked = jnp.concatenate([high, mid], axis=0).astype(jnp.bfloat16)
    by_cols = jnp.dot(stacked, to_rows, preferred_element_type=jnp.float32).astype(jnp.bfloat16)
    side = jnp.concatenate([by_cols[:count], by_cols[count:]], axis=1)
    return jnp.dot(to_slots, side, preferred_element_type=jnp.float32)


def bf16x3_apply(op_high, op_mid, pair, cols):
    both = jnp.dot(op_high, pair, preferred_element_type=jnp.float32)
    return (both[:, :cols] + both[:, cols:]) + jnp.dot(
        op_mid, pair[:, :cols], preferred_element_type=jnp.float32
    )


def body(gap, own_rows, spill_rows, tile_plan, orders, slot_rows):
    order_max = gap.shape[2]
    tile_rows = spill_rows.shape[3]
    own_tiles = own_rows.shape[2] // tile_rows
    hop_span = lax.axis_size("gx") // 4
    own_block = own_rows[0, 0]
    spill_block = spill_rows[0, 0]
    plan_row = tile_plan[0, 0]
    order_now = orders[0, 0]
    slot_map = slot_rows[0, 0]
    row_ids = jnp.arange(order_max, dtype=jnp.int32)
    face_sign = jnp.where(row_ids // (order_max // 4) % 2 == 0, -1.0, 1.0).astype(jnp.float32)
    slot_scale = face_sign * (slot_map < order_now).astype(jnp.float32)
    spill_parts = [spill_block[slot_id] for slot_id in range(2)]
    gap_faces, spill_parts = lax.optimization_barrier((gap[0, 0], spill_parts))
    homed = [
        from_behind(spill_parts[slot_id], "gx", -(slot_id + 1) * hop_span) for slot_id in range(2)
    ]
    own_count = own_block.shape[0]
    cols = gap.shape[3]
    width = order_max // 4
    load = face_sum_parts(
        [gap_faces[face_id * width : (face_id + 1) * width] for face_id in range(4)],
        one_axis_at_a_time=True,
    )
    to_slots = jnp.where(
        slot_map[:, None] == row_ids[None, :], slot_scale[:, None], 0.0
    ).astype(jnp.bfloat16)
    to_rows = jnp.where(
        row_ids[:, None] == slot_map[None, :], slot_scale[None, :], 0.0
    ).astype(jnp.bfloat16)
    own_slots = slot_pieces(own_block, to_rows, to_slots[:, :own_count])
    spill_ids = jnp.concatenate(
        [
            jnp.where(plan_row[slot_id] >= own_tiles, plan_row[slot_id] * tile_rows, -order_max)
            + jnp.arange(tile_rows, dtype=jnp.int32)
            for slot_id in range(2)
        ]
    )
    spill_place = jnp.where(
        slot_map[:, None] == spill_ids[None, :], slot_scale[:, None], 0.0
    ).astype(jnp.bfloat16)
    spill_stack = jnp.concatenate(homed, axis=0)
    spill_slots = slot_pieces(spill_stack, to_rows, spill_place)
    own_high = own_slots[:, :order_max].astype(jnp.bfloat16)
    own_mid = own_slots[:, order_max:].astype(jnp.bfloat16)
    full_slots = own_slots + spill_slots
    op_stack = jnp.concatenate(
        [full_slots[:, :order_max], full_slots[:, order_max:]], axis=0
    ).astype(jnp.bfloat16)
    spill_high = lax.reduce_precision(spill_stack, exponent_bits=8, mantissa_bits=7)
    spill_mid = (spill_stack - spill_high).astype(jnp.bfloat16)
    spill_high = spill_high.astype(jnp.bfloat16)
    centre = (high_bound + low_bound) / 2.0
    half_width = (high_bound - low_bound) / 2.0
    sigma_value = centre / half_width
    rho_value = 1.0 / sigma_value
    solution = jnp.zeros_like(load)
    residual = load
    direction = residual / centre
    for step_id in range(ITERS):
        solution = solution + direction
        dir_high = lax.reduce_precision(direction, exponent_bits=8, mantissa_bits=7)
        dir_pair = jnp.concatenate([dir_high, direction - dir_high], axis=1).astype(jnp.bfloat16)
        if step_id == 0:
            local = bf16x3_apply(own_high, own_mid, dir_pair, cols)
            moved = jnp.dot(to_rows, dir_pair, preferred_element_type=jnp.float32).astype(
                jnp.bfloat16
            )
            spill_out = bf16x3_apply(spill_high, spill_mid, moved, cols)
            out_high = lax.reduce_precision(spill_out, exponent_bits=8, mantissa_bits=7)
            out_rest = spill_out - out_high
            out_mid = lax.reduce_precision(out_rest, exponent_bits=8, mantissa_bits=7)
            pieces = jnp.concatenate([out_high, out_mid, out_rest - out_mid], axis=1)
            placed = jnp.dot(
                spill_place, pieces.astype(jnp.bfloat16), preferred_element_type=jnp.float32
            )
            local = local + (
                (placed[:, :cols] + placed[:, cols : 2 * cols]) + placed[:, 2 * cols :]
            )
        else:
            stacked_out = jnp.dot(op_stack, dir_pair, preferred_element_type=jnp.float32)
            local = (
                stacked_out[:order_max, :cols] + stacked_out[:order_max, cols:]
            ) + stacked_out[order_max:, :cols]
        faces = [local[face_id * width : (face_id + 1) * width] for face_id in range(4)]
        residual = residual - face_sum_parts(faces)
        if step_id + 1 < ITERS:
            rho_next = 1.0 / (2.0 * sigma_value - rho_value)
            direction = rho_next * rho_value * direction + 2.0 * rho_next / half_width * residual
            rho_value = rho_next
    return (solution[None, None], residual[None, None])


def solution(mesh):
    in_specs = (
        P("gx", "gy", None, None),
        P("gx", "gy", None, None),
        P("gx", "gy", None, None, None),
        P("gx", "gy", None),
        P("gx", "gy"),
        P("gx", "gy", None),
    )
    out_specs = (P("gx", "gy", None, None), P("gx", "gy", None, None))
    return jax.shard_map(body, mesh=mesh, in_specs=in_specs, out_specs=out_specs, check_vma=False)
```

```python
import jax
import jax.numpy as jnp
from jax import lax
from jax.sharding import PartitionSpec as P

ITERS = 4


low_bound = 0.5
high_bound = 7.0


def shifted(block, axis, distance):
    devices = range(lax.axis_size(axis))
    route = [(i - distance, i) for i in devices if i - distance in devices]
    return lax.ppermute(block, axis, route)


def from_behind(value, axis, steps):
    count = lax.axis_size(axis)
    pairs = [(source, (source + steps) % count) for source in range(count)]
    return lax.ppermute(value, axis, pairs)


def along_x(part, offset):
    return shifted(part, "gx", offset)


def along_y(part, offset):
    return shifted(part, "gy", offset)


def face_sum(local):
    width = local.shape[0] // 4
    low_x = local[0:width]
    high_x = local[width : 2 * width]
    low_y = local[2 * width : 3 * width]
    high_y = local[3 * width : 4 * width]
    return jnp.concatenate(
        [
            low_x + along_x(high_x, 1),
            high_x + along_x(low_x, -1),
            low_y + along_y(high_y, 1),
            high_y + along_y(low_y, -1),
        ],
        axis=0,
    )


def swap_pairs(count, first):
    pairs = []
    for low in range(first, count - 1, 2):
        pairs += [(low, low + 1), (low + 1, low)]
    return pairs


def face_sum_parts(faces, one_axis_at_a_time=False):
    low_x, high_x, low_y, high_y = faces
    sides = [(low_y, high_y, "gy"), (low_x, high_x, "gx")]
    sends = []
    for low, high, axis in sides:
        even = lax.axis_index(axis) % 2 == 0
        sends.append((jnp.where(even, low, high), swap_pairs(lax.axis_size(axis), 1), axis))
        sends.append((jnp.where(even, high, low), swap_pairs(lax.axis_size(axis), 0), axis))
    if one_axis_at_a_time:
        first = [lax.ppermute(block, axis, pairs) for block, pairs, axis in sends[2:]]
        later, first = lax.optimization_barrier(([block for block, _, _ in sends[:2]], first))
        second = [
            lax.ppermute(block, axis, pairs)
            for block, (_, pairs, axis) in zip(later, sends[:2])
        ]
        received = lax.optimization_barrier(second + first)
    else:
        received = lax.optimization_barrier(
            [lax.ppermute(block, axis, pairs) for block, pairs, axis in sends]
        )
    summed = []
    for side_id, (low, high, axis) in enumerate(sides):
        even = lax.axis_index(axis) % 2 == 0
        odd_recv, even_recv = received[2 * side_id], received[2 * side_id + 1]
        summed.append(low + jnp.where(even, odd_recv, even_recv))
        summed.append(high + jnp.where(even, even_recv, odd_recv))
    new_low_y, new_high_y, new_low_x, new_high_x = summed
    return jnp.concatenate([new_low_x, new_high_x, new_low_y, new_high_y], axis=0)


def slot_pieces(rows, to_rows, to_slots):
    high = lax.reduce_precision(rows, exponent_bits=8, mantissa_bits=7)
    mid = lax.reduce_precision(rows - high, exponent_bits=8, mantissa_bits=7)
    count = rows.shape[0]
    stacked = jnp.concatenate([high, mid], axis=0).astype(jnp.bfloat16)
    by_cols = jnp.dot(stacked, to_rows, preferred_element_type=jnp.float32).astype(jnp.bfloat16)
    side = jnp.concatenate([by_cols[:count], by_cols[count:]], axis=1)
    return jnp.dot(to_slots, side, preferred_element_type=jnp.float32)


def bf16x3_apply(op_high, op_mid, pair, cols):
    both = jnp.dot(op_high, pair, preferred_element_type=jnp.float32)
    return (both[:, :cols] + both[:, cols:]) + jnp.dot(
        op_mid, pair[:, :cols], preferred_element_type=jnp.float32
    )


def body(gap, own_rows, spill_rows, tile_plan, orders, slot_rows):
    order_max = gap.shape[2]
    tile_rows = spill_rows.shape[3]
    own_tiles = own_rows.shape[2] // tile_rows
    hop_span = lax.axis_size("gx") // 4
    own_block = own_rows[0, 0]
    spill_block = spill_rows[0, 0]
    plan_row = tile_plan[0, 0]
    order_now = orders[0, 0]
    slot_map = slot_rows[0, 0]
    row_ids = jnp.arange(order_max, dtype=jnp.int32)
    face_sign = jnp.where(row_ids // (order_max // 4) % 2 == 0, -1.0, 1.0).astype(jnp.float32)
    slot_scale = face_sign * (slot_map < order_now).astype(jnp.float32)
    spill_parts = [spill_block[slot_id] for slot_id in range(2)]
    gap_faces, spill_parts = lax.optimization_barrier((gap[0, 0], spill_parts))
    homed = [
        from_behind(spill_parts[slot_id], "gx", -(slot_id + 1) * hop_span) for slot_id in range(2)
    ]
    own_count = own_block.shape[0]
    cols = gap.shape[3]
    width = order_max // 4
    load = face_sum_parts(
        [gap_faces[face_id * width : (face_id + 1) * width] for face_id in range(4)],
        one_axis_at_a_time=True,
    )
    to_slots = jnp.where(
        slot_map[:, None] == row_ids[None, :], slot_scale[:, None], 0.0
    ).astype(jnp.bfloat16)
    to_rows = jnp.where(
        row_ids[:, None] == slot_map[None, :], slot_scale[None, :], 0.0
    ).astype(jnp.bfloat16)
    own_slots = slot_pieces(own_block, to_rows, to_slots[:, :own_count])
    spill_ids = jnp.concatenate(
        [
            jnp.where(plan_row[slot_id] >= own_tiles, plan_row[slot_id] * tile_rows, -order_max)
            + jnp.arange(tile_rows, dtype=jnp.int32)
            for slot_id in range(2)
        ]
    )
    spill_place = jnp.where(
        slot_map[:, None] == spill_ids[None, :], slot_scale[:, None], 0.0
    ).astype(jnp.bfloat16)
    spill_stack = jnp.concatenate(homed, axis=0)
    spill_slots = slot_pieces(spill_stack, to_rows, spill_place)
    own_high = own_slots[:, :order_max].astype(jnp.bfloat16)
    own_mid = own_slots[:, order_max:].astype(jnp.bfloat16)
    full_slots = own_slots + spill_slots
    op_stack = jnp.concatenate(
        [full_slots[:, :order_max], full_slots[:, order_max:]], axis=0
    ).astype(jnp.bfloat16)
    spill_high = lax.reduce_precision(spill_stack, exponent_bits=8, mantissa_bits=7)
    spill_both = jnp.concatenate([spill_high, spill_stack - spill_high], axis=0).astype(
        jnp.bfloat16
    )
    spill_count = spill_stack.shape[0]
    centre = (high_bound + low_bound) / 2.0
    half_width = (high_bound - low_bound) / 2.0
    sigma_value = centre / half_width
    rho_value = 1.0 / sigma_value
    solution = jnp.zeros_like(load)
    residual = load
    direction = residual / centre
    for step_id in range(ITERS):
        solution = solution + direction
        dir_high = lax.reduce_precision(direction, exponent_bits=8, mantissa_bits=7)
        dir_pair = jnp.concatenate([dir_high, direction - dir_high], axis=1).astype(jnp.bfloat16)
        if step_id == 0:
            local = bf16x3_apply(own_high, own_mid, dir_pair, cols)
            moved = jnp.dot(to_rows, dir_pair, preferred_element_type=jnp.float32).astype(
                jnp.bfloat16
            )
            spill_prod = jnp.dot(spill_both, moved, preferred_element_type=jnp.float32)
            spill_out = (
                spill_prod[:spill_count, :cols] + spill_prod[:spill_count, cols:]
            ) + spill_prod[spill_count:, :cols]
            out_high = lax.reduce_precision(spill_out, exponent_bits=8, mantissa_bits=7)
            out_rest = spill_out - out_high
            out_mid = lax.reduce_precision(out_rest, exponent_bits=8, mantissa_bits=7)
            pieces = jnp.concatenate([out_high, out_mid, out_rest - out_mid], axis=1)
            placed = jnp.dot(
                spill_place, pieces.astype(jnp.bfloat16), preferred_element_type=jnp.float32
            )
            local = local + (
                (placed[:, :cols] + placed[:, cols : 2 * cols]) + placed[:, 2 * cols :]
            )
        else:
            stacked_out = jnp.dot(op_stack, dir_pair, preferred_element_type=jnp.float32)
            local = (
                stacked_out[:order_max, :cols] + stacked_out[:order_max, cols:]
            ) + stacked_out[order_max:, :cols]
        faces = [local[face_id * width : (face_id + 1) * width] for face_id in range(4)]
        residual = residual - face_sum_parts(faces)
        if step_id + 1 < ITERS:
            rho_next = 1.0 / (2.0 * sigma_value - rho_value)
            direction = rho_next * rho_value * direction + 2.0 * rho_next / half_width * residual
            rho_value = rho_next
    return (solution[None, None], residual[None, None])


def solution(mesh):
    in_specs = (
        P("gx", "gy", None, None),
        P("gx", "gy", None, None),
        P("gx", "gy", None, None, None),
        P("gx", "gy", None),
        P("gx", "gy"),
        P("gx", "gy", None),
    )
    out_specs = (P("gx", "gy", None, None), P("gx", "gy", None, None))
    return jax.shard_map(body, mesh=mesh, in_specs=in_specs, out_specs=out_specs, check_vma=False)
```

```python
import jax
import jax.numpy as jnp
from jax import lax
from jax.sharding import PartitionSpec as P

ITERS = 4


low_bound = 0.5
high_bound = 7.0


def shifted(block, axis, distance):
    devices = range(lax.axis_size(axis))
    route = [(i - distance, i) for i in devices if i - distance in devices]
    return lax.ppermute(block, axis, route)


def from_behind(value, axis, steps):
    count = lax.axis_size(axis)
    pairs = [(source, (source + steps) % count) for source in range(count)]
    return lax.ppermute(value, axis, pairs)


def along_x(part, offset):
    return shifted(part, "gx", offset)


def along_y(part, offset):
    return shifted(part, "gy", offset)


def face_sum(local):
    width = local.shape[0] // 4
    low_x = local[0:width]
    high_x = local[width : 2 * width]
    low_y = local[2 * width : 3 * width]
    high_y = local[3 * width : 4 * width]
    return jnp.concatenate(
        [
            low_x + along_x(high_x, 1),
            high_x + along_x(low_x, -1),
            low_y + along_y(high_y, 1),
            high_y + along_y(low_y, -1),
        ],
        axis=0,
    )


def swap_pairs(count, first):
    pairs = []
    for low in range(first, count - 1, 2):
        pairs += [(low, low + 1), (low + 1, low)]
    return pairs


def face_sum_parts(faces, one_axis_at_a_time=False):
    low_x, high_x, low_y, high_y = faces
    sides = [(low_y, high_y, "gy"), (low_x, high_x, "gx")]
    sends = []
    for low, high, axis in sides:
        even = lax.axis_index(axis) % 2 == 0
        sends.append((jnp.where(even, low, high), swap_pairs(lax.axis_size(axis), 1), axis))
        sends.append((jnp.where(even, high, low), swap_pairs(lax.axis_size(axis), 0), axis))
    if one_axis_at_a_time:
        first = [lax.ppermute(block, axis, pairs) for block, pairs, axis in sends[2:]]
        later, first = lax.optimization_barrier(([block for block, _, _ in sends[:2]], first))
        second = [
            lax.ppermute(block, axis, pairs)
            for block, (_, pairs, axis) in zip(later, sends[:2])
        ]
        received = lax.optimization_barrier(second + first)
    else:
        received = lax.optimization_barrier(
            [lax.ppermute(block, axis, pairs) for block, pairs, axis in sends]
        )
    summed = []
    for side_id, (low, high, axis) in enumerate(sides):
        even = lax.axis_index(axis) % 2 == 0
        odd_recv, even_recv = received[2 * side_id], received[2 * side_id + 1]
        summed.append(low + jnp.where(even, odd_recv, even_recv))
        summed.append(high + jnp.where(even, even_recv, odd_recv))
    new_low_y, new_high_y, new_low_x, new_high_x = summed
    return jnp.concatenate([new_low_x, new_high_x, new_low_y, new_high_y], axis=0)


def slot_pieces(rows, to_rows, to_slots):
    high = lax.reduce_precision(rows, exponent_bits=8, mantissa_bits=7)
    mid = lax.reduce_precision(rows - high, exponent_bits=8, mantissa_bits=7)
    count = rows.shape[0]
    stacked = jnp.concatenate([high, mid], axis=0).astype(jnp.bfloat16)
    by_cols = jnp.dot(stacked, to_rows, preferred_element_type=jnp.float32).astype(jnp.bfloat16)
    side = jnp.concatenate([by_cols[:count], by_cols[count:]], axis=1)
    return jnp.dot(to_slots, side, preferred_element_type=jnp.float32)


def bf16x3_apply(op_high, op_mid, pair, cols):
    both = jnp.dot(op_high, pair, preferred_element_type=jnp.float32)
    return (both[:, :cols] + both[:, cols:]) + jnp.dot(
        op_mid, pair[:, :cols], preferred_element_type=jnp.float32
    )


def body(gap, own_rows, spill_rows, tile_plan, orders, slot_rows):
    order_max = gap.shape[2]
    tile_rows = spill_rows.shape[3]
    own_tiles = own_rows.shape[2] // tile_rows
    hop_span = lax.axis_size("gx") // 4
    own_block = own_rows[0, 0]
    spill_block = spill_rows[0, 0]
    plan_row = tile_plan[0, 0]
    order_now = orders[0, 0]
    slot_map = slot_rows[0, 0]
    row_ids = jnp.arange(order_max, dtype=jnp.int32)
    face_sign = jnp.where(row_ids // (order_max // 4) % 2 == 0, -1.0, 1.0).astype(jnp.float32)
    slot_scale = face_sign * (slot_map < order_now).astype(jnp.float32)
    spill_parts = [spill_block[slot_id] for slot_id in range(2)]
    gap_faces, spill_parts = lax.optimization_barrier((gap[0, 0], spill_parts))
    homed = [
        from_behind(spill_parts[slot_id], "gx", -(slot_id + 1) * hop_span) for slot_id in range(2)
    ]
    own_count = own_block.shape[0]
    cols = gap.shape[3]
    width = order_max // 4
    load = face_sum_parts(
        [gap_faces[face_id * width : (face_id + 1) * width] for face_id in range(4)],
        one_axis_at_a_time=True,
    )
    to_slots = jnp.where(
        slot_map[:, None] == row_ids[None, :], slot_scale[:, None], 0.0
    ).astype(jnp.bfloat16)
    to_rows = jnp.where(
        row_ids[:, None] == slot_map[None, :], slot_scale[None, :], 0.0
    ).astype(jnp.bfloat16)
    own_slots = slot_pieces(own_block, to_rows, to_slots[:, :own_count])
    spill_ids = jnp.concatenate(
        [
            jnp.where(plan_row[slot_id] >= own_tiles, plan_row[slot_id] * tile_rows, -order_max)
            + jnp.arange(tile_rows, dtype=jnp.int32)
            for slot_id in range(2)
        ]
    )
    spill_place = jnp.where(
        slot_map[:, None] == spill_ids[None, :], slot_scale[:, None], 0.0
    ).astype(jnp.bfloat16)
    spill_stack = jnp.concatenate(homed, axis=0)
    spill_slots = slot_pieces(spill_stack, to_rows, spill_place)
    own_high = own_slots[:, :order_max].astype(jnp.bfloat16)
    own_mid = own_slots[:, order_max:].astype(jnp.bfloat16)
    full_slots = own_slots + spill_slots
    op_stack = jnp.concatenate(
        [full_slots[:, :order_max], full_slots[:, order_max:]], axis=0
    ).astype(jnp.bfloat16)
    spill_high = lax.reduce_precision(spill_stack, exponent_bits=8, mantissa_bits=7)
    spill_mid = (spill_stack - spill_high).astype(jnp.bfloat16)
    spill_high = spill_high.astype(jnp.bfloat16)
    centre = (high_bound + low_bound) / 2.0
    half_width = (high_bound - low_bound) / 2.0
    sigma_value = centre / half_width
    rho_value = 1.0 / sigma_value
    solution = jnp.zeros_like(load)
    residual = load
    direction = residual / centre
    for step_id in range(ITERS):
        if step_id + 1 == ITERS:
            residual = lax.optimization_barrier(residual)
        solution = solution + direction
        dir_high = lax.reduce_precision(direction, exponent_bits=8, mantissa_bits=7)
        dir_pair = jnp.concatenate([dir_high, direction - dir_high], axis=1).astype(jnp.bfloat16)
        if step_id == 0:
            local = bf16x3_apply(own_high, own_mid, dir_pair, cols)
            moved = jnp.dot(to_rows, dir_pair, preferred_element_type=jnp.float32).astype(
                jnp.bfloat16
            )
            spill_out = bf16x3_apply(spill_high, spill_mid, moved, cols)
            out_high = lax.reduce_precision(spill_out, exponent_bits=8, mantissa_bits=7)
            out_rest = spill_out - out_high
            out_mid = lax.reduce_precision(out_rest, exponent_bits=8, mantissa_bits=7)
            pieces = jnp.concatenate([out_high, out_mid, out_rest - out_mid], axis=1)
            placed = jnp.dot(
                spill_place, pieces.astype(jnp.bfloat16), preferred_element_type=jnp.float32
            )
            local = local + (
                (placed[:, :cols] + placed[:, cols : 2 * cols]) + placed[:, 2 * cols :]
            )
        else:
            stacked_out = jnp.dot(op_stack, dir_pair, preferred_element_type=jnp.float32)
            local = (
                stacked_out[:order_max, :cols] + stacked_out[:order_max, cols:]
            ) + stacked_out[order_max:, :cols]
        faces = [local[face_id * width : (face_id + 1) * width] for face_id in range(4)]
        residual = residual - face_sum_parts(faces)
        if step_id + 1 < ITERS:
            rho_next = 1.0 / (2.0 * sigma_value - rho_value)
            direction = rho_next * rho_value * direction + 2.0 * rho_next / half_width * residual
            rho_value = rho_next
    return (solution[None, None], residual[None, None])


def solution(mesh):
    in_specs = (
        P("gx", "gy", None, None),
        P("gx", "gy", None, None),
        P("gx", "gy", None, None, None),
        P("gx", "gy", None),
        P("gx", "gy"),
        P("gx", "gy", None),
    )
    out_specs = (P("gx", "gy", None, None), P("gx", "gy", None, None))
    return jax.shard_map(body, mesh=mesh, in_specs=in_specs, out_specs=out_specs, check_vma=False)
```

```python
import jax
import jax.numpy as jnp
from jax import lax
from jax.sharding import PartitionSpec as P

ITERS = 4


low_bound = 0.5
high_bound = 7.0


def shifted(block, axis, distance):
    devices = range(lax.axis_size(axis))
    route = [(i - distance, i) for i in devices if i - distance in devices]
    return lax.ppermute(block, axis, route)


def from_behind(value, axis, steps):
    count = lax.axis_size(axis)
    pairs = [(source, (source + steps) % count) for source in range(count)]
    return lax.ppermute(value, axis, pairs)


def along_x(part, offset):
    return shifted(part, "gx", offset)


def along_y(part, offset):
    return shifted(part, "gy", offset)


def face_sum(local):
    width = local.shape[0] // 4
    low_x = local[0:width]
    high_x = local[width : 2 * width]
    low_y = local[2 * width : 3 * width]
    high_y = local[3 * width : 4 * width]
    return jnp.concatenate(
        [
            low_x + along_x(high_x, 1),
            high_x + along_x(low_x, -1),
            low_y + along_y(high_y, 1),
            high_y + along_y(low_y, -1),
        ],
        axis=0,
    )


def swap_pairs(count, first):
    pairs = []
    for low in range(first, count - 1, 2):
        pairs += [(low, low + 1), (low + 1, low)]
    return pairs


def face_sum_parts(faces, one_axis_at_a_time=False):
    low_x, high_x, low_y, high_y = faces
    sides = [(low_y, high_y, "gy"), (low_x, high_x, "gx")]
    sends = []
    for low, high, axis in sides:
        even = lax.axis_index(axis) % 2 == 0
        sends.append((jnp.where(even, low, high), swap_pairs(lax.axis_size(axis), 1), axis))
        sends.append((jnp.where(even, high, low), swap_pairs(lax.axis_size(axis), 0), axis))
    if one_axis_at_a_time:
        first = [lax.ppermute(block, axis, pairs) for block, pairs, axis in sends[2:]]
        later, first = lax.optimization_barrier(([block for block, _, _ in sends[:2]], first))
        second = [
            lax.ppermute(block, axis, pairs)
            for block, (_, pairs, axis) in zip(later, sends[:2])
        ]
        received = lax.optimization_barrier(second + first)
    else:
        received = lax.optimization_barrier(
            [lax.ppermute(block, axis, pairs) for block, pairs, axis in sends]
        )
    summed = []
    for side_id, (low, high, axis) in enumerate(sides):
        even = lax.axis_index(axis) % 2 == 0
        odd_recv, even_recv = received[2 * side_id], received[2 * side_id + 1]
        summed.append(low + jnp.where(even, odd_recv, even_recv))
        summed.append(high + jnp.where(even, even_recv, odd_recv))
    new_low_y, new_high_y, new_low_x, new_high_x = summed
    return jnp.concatenate([new_low_x, new_high_x, new_low_y, new_high_y], axis=0)


def slot_pieces(rows, to_rows, to_slots):
    high = lax.reduce_precision(rows, exponent_bits=8, mantissa_bits=7)
    mid = lax.reduce_precision(rows - high, exponent_bits=8, mantissa_bits=7)
    count = rows.shape[0]
    stacked = jnp.concatenate([high, mid], axis=0).astype(jnp.bfloat16)
    by_cols = jnp.dot(stacked, to_rows, preferred_element_type=jnp.float32).astype(jnp.bfloat16)
    side = jnp.concatenate([by_cols[:count], by_cols[count:]], axis=1)
    return jnp.dot(to_slots, side, preferred_element_type=jnp.float32)


def bf16x3_apply(op_high, op_mid, pair, cols):
    both = jnp.dot(op_high, pair, preferred_element_type=jnp.float32)
    return (both[:, :cols] + both[:, cols:]) + jnp.dot(
        op_mid, pair[:, :cols], preferred_element_type=jnp.float32
    )


def body(gap, own_rows, spill_rows, tile_plan, orders, slot_rows):
    order_max = gap.shape[2]
    tile_rows = spill_rows.shape[3]
    own_tiles = own_rows.shape[2] // tile_rows
    hop_span = lax.axis_size("gx") // 4
    own_block = own_rows[0, 0]
    spill_block = spill_rows[0, 0]
    plan_row = tile_plan[0, 0]
    order_now = orders[0, 0]
    slot_map = slot_rows[0, 0]
    row_ids = jnp.arange(order_max, dtype=jnp.int32)
    face_sign = jnp.where(row_ids // (order_max // 4) % 2 == 0, -1.0, 1.0).astype(jnp.float32)
    slot_scale = face_sign * (slot_map < order_now).astype(jnp.float32)
    spill_parts = [spill_block[slot_id] for slot_id in range(2)]
    gap_faces, spill_parts = lax.optimization_barrier((gap[0, 0], spill_parts))
    homed = [
        from_behind(spill_parts[slot_id], "gx", -(slot_id + 1) * hop_span) for slot_id in range(2)
    ]
    own_count = own_block.shape[0]
    cols = gap.shape[3]
    width = order_max // 4
    load = face_sum_parts(
        [gap_faces[face_id * width : (face_id + 1) * width] for face_id in range(4)],
        one_axis_at_a_time=True,
    )
    to_slots = jnp.where(
        slot_map[:, None] == row_ids[None, :], slot_scale[:, None], 0.0
    ).astype(jnp.bfloat16)
    to_rows = jnp.where(
        row_ids[:, None] == slot_map[None, :], slot_scale[None, :], 0.0
    ).astype(jnp.bfloat16)
    own_slots = slot_pieces(own_block, to_rows, to_slots[:, :own_count])
    spill_ids = jnp.concatenate(
        [
            jnp.where(plan_row[slot_id] >= own_tiles, plan_row[slot_id] * tile_rows, -order_max)
            + jnp.arange(tile_rows, dtype=jnp.int32)
            for slot_id in range(2)
        ]
    )
    spill_place = jnp.where(
        slot_map[:, None] == spill_ids[None, :], slot_scale[:, None], 0.0
    ).astype(jnp.bfloat16)
    spill_slots = [
        slot_pieces(homed[slot_id], to_rows, spill_place[:, slot_id * tile_rows : (slot_id + 1) * tile_rows])
        for slot_id in range(2)
    ]
    own_high = own_slots[:, :order_max].astype(jnp.bfloat16)
    own_mid = own_slots[:, order_max:].astype(jnp.bfloat16)
    full_slots = own_slots + (spill_slots[0] + spill_slots[1])
    op_stack = jnp.concatenate(
        [full_slots[:, :order_max], full_slots[:, order_max:]], axis=0
    ).astype(jnp.bfloat16)
    spill_high = [lax.reduce_precision(block, exponent_bits=8, mantissa_bits=7) for block in homed]
    spill_mid = [(block - high).astype(jnp.bfloat16) for block, high in zip(homed, spill_high)]
    spill_high = [high.astype(jnp.bfloat16) for high in spill_high]
    centre = (high_bound + low_bound) / 2.0
    half_width = (high_bound - low_bound) / 2.0
    sigma_value = centre / half_width
    rho_value = 1.0 / sigma_value
    solution = jnp.zeros_like(load)
    residual = load
    direction = residual / centre
    for step_id in range(ITERS):
        solution = solution + direction
        dir_high = lax.reduce_precision(direction, exponent_bits=8, mantissa_bits=7)
        dir_pair = jnp.concatenate([dir_high, direction - dir_high], axis=1).astype(jnp.bfloat16)
        if step_id == 0:
            local = bf16x3_apply(own_high, own_mid, dir_pair, cols)
            moved = jnp.dot(to_rows, dir_pair, preferred_element_type=jnp.float32).astype(
                jnp.bfloat16
            )
            for slot_id in range(2):
                spill_out = bf16x3_apply(spill_high[slot_id], spill_mid[slot_id], moved, cols)
                out_high = lax.reduce_precision(spill_out, exponent_bits=8, mantissa_bits=7)
                out_rest = spill_out - out_high
                out_mid = lax.reduce_precision(out_rest, exponent_bits=8, mantissa_bits=7)
                pieces = jnp.concatenate([out_high, out_mid, out_rest - out_mid], axis=1)
                placed = jnp.dot(
                    spill_place[:, slot_id * tile_rows : (slot_id + 1) * tile_rows],
                    pieces.astype(jnp.bfloat16),
                    preferred_element_type=jnp.float32,
                )
                local = local + (
                    (placed[:, :cols] + placed[:, cols : 2 * cols]) + placed[:, 2 * cols :]
                )
        else:
            stacked_out = jnp.dot(op_stack, dir_pair, preferred_element_type=jnp.float32)
            local = (
                stacked_out[:order_max, :cols] + stacked_out[:order_max, cols:]
            ) + stacked_out[order_max:, :cols]
        faces = [local[face_id * width : (face_id + 1) * width] for face_id in range(4)]
        residual = residual - face_sum_parts(faces)
        if step_id + 1 < ITERS:
            rho_next = 1.0 / (2.0 * sigma_value - rho_value)
            direction = rho_next * rho_value * direction + 2.0 * rho_next / half_width * residual
            rho_value = rho_next
    return (solution[None, None], residual[None, None])


def solution(mesh):
    in_specs = (
        P("gx", "gy", None, None),
        P("gx", "gy", None, None),
        P("gx", "gy", None, None, None),
        P("gx", "gy", None),
        P("gx", "gy"),
        P("gx", "gy", None),
    )
    out_specs = (P("gx", "gy", None, None), P("gx", "gy", None, None))
    return jax.shard_map(body, mesh=mesh, in_specs=in_specs, out_specs=out_specs, check_vma=False)
```
